512 devices in a mesh: atom: 64 (over y, x, z_hi), ka: 8 (over z_lo, core).
Axes of the slice: x: 4, y: 8, z: 8 (z_hi: 2, z_lo: 4; z = z_hi * 4 + z_lo), core: 2. Of those that a mesh axis runs over, the one named last changes fastest.
Arguments:
- features: bfloat16 [131072, 256], P('atom'), may hold values from -6 to 6
- positions: float32 [3, 131072], P(None, 'atom'), may hold values from 0 to 1
- k_indices: int32 [3, 4096], P(None, 'ka'), may hold values from -8 to 8
- species: int32 [131072], P('atom'), may hold values from 0 to 7
- brick_counts: int32 [64], P('atom'), may hold values from 1024 to 2048, as said below
- smearing: float32 [256], replicated, may hold values from 0.01 to 0.03
- teacher_charge: float32 [256], replicated, may hold values from -0.375 to 0.375
- norm_gain: float32 [256], replicated, may hold values from 0.5 to 1.5
- w_mix: bfloat16 [256, 256], replicated, may hold values from -0.375 to 0.375
- w_read: float32 [256], replicated, may hold values from -0.375 to 0.375
- w_student: bfloat16 [256, 128], replicated, may hold values from -0.375 to 0.375
- species_embed: float32 [8, 128], replicated, may hold values from -3 to 3
- w_charge: float32 [128], replicated, may hold values from -0.5 to 0.5
- species_bias: float32 [8], replicated, may hold values from -3 to 3
- student_smear: float32 [1], replicated, may hold values from 0.05 to 0.15
Outputs:
- teacher_features: bfloat16 [131072, 256], P(('atom', 'ka'))
- teacher_forces: float32 [3, 131072], P(None, ('atom', 'ka'))
- student_forces: float32 [3, 131072], P(None, ('atom', 'ka'))
- student_energy: float32 [131072], P(('atom', 'ka'))
- distill_loss: float32 [], replicated
The draws below stay inside these ranges and needn't reach their ends.
Inputs may be any that keep to these rules, and one draw needn't show every extreme that they name: The first brick_counts[b] atom slots of brick b hold real atoms and the rest are padding; some brick is full in every draw.
All inputs are finite; a program needn't handle non-finite values.
Results may differ from the reference program's by a relative error of at most 0.0075.
Values sent between devices are 32-bit elements; how exact they have to be, the bound alone decides.
No kernel may reach another device: no remote copies, remote signals or barrier semaphores. Data moves between devices by JAX's collectives and lax.ppermute only.
A program may use at most 64 MiB of HBM per device.

```python
import math
import jax
import jax.numpy as jnp
from jax import lax

C = 256
KVEC = 4096
HS = 128
NSPEC = 8
A_DEV = 2048
BRICKS = 64
ATOMS = 131072


def draw_brick_counts(key, part):
    counts = jax.random.randint(jax.random.fold_in(key, 11), (BRICKS,), A_DEV // 2, A_DEV + 1)
    chosen = jax.random.randint(jax.random.fold_in(key, 12), (), 0, BRICKS)
    return jnp.where(jnp.arange(BRICKS) == chosen, A_DEV, counts).astype(jnp.int32)


def plant(entries, stream_key, smallest, high):
    dims = entries.shape
    place = [jax.random.randint(jax.random.fold_in(stream_key, axis), (), 0, dims[axis]) for axis in range(len(dims))]
    entries = entries.at[tuple(place)].set(smallest)
    longest = dims.index(max(dims))
    place[longest] = (place[longest] + 1) % dims[longest]
    return entries.at[tuple(place)].set(high)


def block_levels(key, shape, shards, smallest, largest):
    def one(axis_at, parts):
        draws = jax.random.uniform(jax.random.fold_in(jax.random.fold_in(key, 6), axis_at), (parts,), jnp.float32, smallest / len(shards), largest / len(shards))
        return jnp.repeat(jnp.exp(draws), shape[axis_at] // parts).reshape((-1,) + (1,) * (len(shape) - axis_at - 1))

    factor_of = one(*shards[0])
    for cut in shards[1:]:
        factor_of = factor_of * one(*cut)
    return factor_of


def gaussian(own_key, shape, scale, limit, pieces=(), kind=jnp.bfloat16):
    array = scale * jax.random.normal(own_key, shape, jnp.float32)
    if pieces:
        array = array * block_levels(own_key, shape, pieces, -0.22, 0.18)
    return jnp.clip(array, -limit, limit).astype(kind)


def setup_inputs(seed: int = 0) -> dict:
    splits = jax.random.split(jax.random.key(seed), 16)
    return {
        "features": gaussian(splits[0], (ATOMS, C), 1.0, 6.0, ((0, 64),)),
        "positions": jnp.clip(1.0 * jax.random.uniform(splits[1], (3, ATOMS), jnp.float32) ** block_levels(splits[1], (3, ATOMS), ((1, 64),), -0.2, 0.2), 0.0, 1.0),
        "k_indices": plant(jax.random.randint(splits[2], (3, KVEC), -8, 9), jax.random.fold_in(splits[2], 1), -8, 8).astype(jnp.int32),
        "species": plant(jax.random.randint(splits[3], (ATOMS,), 0, NSPEC), jax.random.fold_in(splits[3], 1), 0, NSPEC - 1).astype(jnp.int32),
        "brick_counts": draw_brick_counts(jax.random.fold_in(splits[15], 71), 0),
        "smearing": jnp.clip(jnp.exp(jax.random.uniform(splits[5], (C,), jnp.float32, math.log(0.01), math.log(0.03))), 0.01, 0.03),
        "teacher_charge": gaussian(splits[6], (C,), C ** -0.5, 0.375, (), jnp.float32),
        "norm_gain": jnp.clip(1.0 + 0.1 * jax.random.normal(splits[7], (C,), jnp.float32), 0.5, 1.5),
        "w_mix": gaussian(splits[8], (C, C), C ** -0.5, 0.375),
        "w_read": gaussian(splits[9], (C,), C ** -0.5, 0.375, (), jnp.float32),
        "w_student": gaussian(splits[10], (C, HS), C ** -0.5, 0.375),
        "species_embed": gaussian(splits[11], (NSPEC, HS), 0.5, 3.0, (), jnp.float32),
        "w_charge": gaussian(splits[12], (HS,), HS ** -0.5, 0.5, (), jnp.float32),
        "species_bias": gaussian(splits[13], (NSPEC,), 0.5, 3.0, (), jnp.float32),
        "student_smear": jnp.clip(jnp.exp(jax.random.uniform(splits[14], (1,), jnp.float32, math.log(0.05), math.log(0.15))), 0.05, 0.15),
    }


TWO_PI = 2.0 * math.pi
SCREEN = 20.0
HIGHEST_PRECISION = lax.Precision.HIGHEST

def phase_table(positions, k_indices):
    k_float = k_indices.astype(jnp.float32)
    products = positions[0][:, None] * k_float[0][None, :] + positions[1][:, None] * k_float[1][None, :] + positions[2][:, None] * k_float[2][None, :]
    angles = TWO_PI * products
    return jnp.concatenate([jnp.cos(angles), jnp.sin(angles)], axis=1).astype(jnp.bfloat16)

def k_geometry(k_indices):
    k_vectors = TWO_PI * k_indices.astype(jnp.float32)
    k_square = k_vectors[0] * k_vectors[0] + k_vectors[1] * k_vectors[1] + k_vectors[2] * k_vectors[2]
    return (k_vectors, k_square)

def teacher_kernel(k_square, smearing, inv_root):
    spread = (smearing * smearing)[None, :]
    return jnp.exp(-0.5 * k_square[:, None] * spread) / (k_square[:, None] + SCREEN) * inv_root

def student_table(k_vectors, k_square, sums, student_smear, inv_root, k_width):
    spread = student_smear[0] * student_smear[0]
    kernel = jnp.exp(-0.5 * k_square * spread) / (k_square + SCREEN) * inv_root
    cos_part = kernel * sums[:k_width]
    sin_part = kernel * sums[k_width:]
    upper_rows = jnp.stack([cos_part, -(k_vectors[0] * sin_part), -(k_vectors[1] * sin_part), -(k_vectors[2] * sin_part)], axis=1)
    lower_rows = jnp.stack([sin_part, k_vectors[0] * cos_part, k_vectors[1] * cos_part, k_vectors[2] * cos_part], axis=1)
    return jnp.concatenate([upper_rows, lower_rows], axis=0).astype(jnp.bfloat16)

def student_charge(features, species, live_mask, w_student, species_embed, w_charge, species_bias):
    onehot = (species[:, None] == jnp.arange(species_embed.shape[0], dtype=jnp.int32)[None, :]).astype(jnp.float32)
    inner_sum = jnp.dot(features, w_student, preferred_element_type=jnp.float32) + jnp.dot(onehot, species_embed, precision=HIGHEST_PRECISION)
    hidden = jax.nn.silu(inner_sum)
    return (jnp.dot(hidden, w_charge, precision=HIGHEST_PRECISION) + jnp.dot(onehot, species_bias, precision=HIGHEST_PRECISION)) * live_mask

def finish(potential, teacher_force, student_part, features, charge, live_mask, norm_gain, w_mix, w_read):
    mean_square = lax.optimization_barrier(jnp.mean(potential * potential, axis=1, keepdims=True))
    normed = (potential * lax.rsqrt(mean_square + 1e-06) * norm_gain[None, :]).astype(jnp.bfloat16)
    update = jax.nn.silu(jnp.dot(normed, w_mix, preferred_element_type=jnp.float32))
    combined = features.astype(jnp.float32) + update
    teacher_energy = jnp.dot(combined, w_read, precision=HIGHEST_PRECISION)
    student_energy = 0.5 * charge * student_part[:, 0]
    forces = charge[:, None] * student_part[:, 1:4]
    misfit = (student_energy - teacher_energy) ** 2 + lax.optimization_barrier(jnp.sum((forces - teacher_force) ** 2, axis=1)) / 3.0
    return (combined.astype(jnp.bfloat16), teacher_force, forces, student_energy, live_mask * misfit)

def reference(features, positions, k_indices, species, brick_counts, smearing, teacher_charge, norm_gain, w_mix, w_read, w_student, species_embed, w_charge, species_bias, student_smear):
    inv_root = 1.0 / math.sqrt(ATOMS)
    atom_ids = jnp.arange(ATOMS, dtype=jnp.int32)
    live_mask = (atom_ids % A_DEV < jnp.repeat(brick_counts, A_DEV)).astype(jnp.float32)
    masked = features * live_mask.astype(jnp.bfloat16)[:, None]
    charge = student_charge(features, species, live_mask, w_student, species_embed, w_charge, species_bias)
    charge_low = charge.astype(jnp.bfloat16)
    charged = (features.astype(jnp.float32) * teacher_charge[None, :]).astype(jnp.bfloat16)
    k_width = min(512, KVEC)
    k_blocks = KVEC // k_width
    blocked = k_indices.reshape(3, k_blocks, k_width).transpose(1, 0, 2)

    def sums_of(k_block):
        phases = phase_table(positions, k_block)
        factor = lax.dot_general(phases, masked, (((0,), (0,)), ((), ())), preferred_element_type=jnp.float32)
        charge_sum = jnp.dot(charge_low, phases, preferred_element_type=jnp.float32)
        return (factor, charge_sum)
    factors, charge_sums = lax.map(sums_of, blocked)

    def accumulate(running, inputs):
        k_block, factor, charge_sum = inputs
        potential, teacher_force, student_part = running
        phases = phase_table(positions, k_block)
        k_vectors, k_square = k_geometry(k_block)
        kernel = teacher_kernel(k_square, smearing, inv_root)
        weighted = (jnp.concatenate([kernel, kernel], axis=0) * factor).astype(jnp.bfloat16)
        potential = potential + jnp.dot(phases, weighted, preferred_element_type=jnp.float32)
        contracted = lax.dot_general(charged, weighted, (((1,), (1,)), ((), ())), preferred_element_type=jnp.float32)
        cosines = phases[:, :k_width].astype(jnp.float32)
        sines = phases[:, k_width:].astype(jnp.float32)
        force_terms = sines * contracted[:, :k_width] - cosines * contracted[:, k_width:]
        teacher_force = teacher_force + jnp.dot(force_terms, k_vectors.T, precision=HIGHEST_PRECISION)
        table = student_table(k_vectors, k_square, charge_sum, student_smear, inv_root, k_width)
        student_part = student_part + jnp.dot(phases, table, preferred_element_type=jnp.float32)
        return ((potential, teacher_force, student_part), None)
    start_state = (jnp.zeros((ATOMS, C), jnp.float32), jnp.zeros((ATOMS, 3), jnp.float32), jnp.zeros((ATOMS, 4), jnp.float32))
    (potential, teacher_force, student_part), unused = lax.scan(accumulate, start_state, (blocked, factors, charge_sums))
    teacher_features, teacher_out, forces, student_energy, misfit = finish(potential, teacher_force, student_part, features, charge, live_mask, norm_gain, w_mix, w_read)
    distill_loss = jnp.sum(misfit) / jnp.sum(live_mask)
    return (teacher_features, teacher_out.T, forces.T, student_energy, distill_loss)
```

```python
import functools
import math

import jax
import jax.numpy as jnp
from jax import lax
from jax.sharding import Mesh
from jax.sharding import PartitionSpec as P

TWO_PI = 2.0 * math.pi
SCREEN = 20.0
HIGHEST_PRECISION = lax.Precision.HIGHEST

ATOM_AXES = ("y", "x", "zh")
KA_AXES = ("zl", "core")
ALL_AXES = ATOM_AXES + KA_AXES
PAD_ROWS = 256


def phase_table(positions, k_indices):
    k_float = k_indices.astype(jnp.float32)
    products = (
        positions[0][:, None] * k_float[0][None, :]
        + positions[1][:, None] * k_float[1][None, :]
        + positions[2][:, None] * k_float[2][None, :]
    )
    angles = TWO_PI * products
    return jnp.concatenate([jnp.cos(angles), jnp.sin(angles)], axis=1).astype(jnp.bfloat16)


def k_geometry(k_indices):
    k_vectors = TWO_PI * k_indices.astype(jnp.float32)
    k_square = (
        k_vectors[0] * k_vectors[0] + k_vectors[1] * k_vectors[1] + k_vectors[2] * k_vectors[2]
    )
    return (k_vectors, k_square)


def teacher_kernel(k_square, smearing, inv_root):
    spread = (smearing * smearing)[None, :]
    return jnp.exp(-0.5 * k_square[:, None] * spread) / (k_square[:, None] + SCREEN) * inv_root


def student_table(k_vectors, k_square, sums, student_smear, inv_root, k_width):
    spread = student_smear[0] * student_smear[0]
    kernel = jnp.exp(-0.5 * k_square * spread) / (k_square + SCREEN) * inv_root
    cos_part = kernel * sums[:k_width]
    sin_part = kernel * sums[k_width:]
    upper_rows = jnp.stack(
        [
            cos_part,
            -(k_vectors[0] * sin_part),
            -(k_vectors[1] * sin_part),
            -(k_vectors[2] * sin_part),
        ],
        axis=1,
    )
    lower_rows = jnp.stack(
        [sin_part, k_vectors[0] * cos_part, k_vectors[1] * cos_part, k_vectors[2] * cos_part],
        axis=1,
    )
    return jnp.concatenate([upper_rows, lower_rows], axis=0).astype(jnp.bfloat16)


def student_charge(features, species, live_mask, w_student, species_embed, w_charge, species_bias):
    onehot = (
        species[:, None] == jnp.arange(species_embed.shape[0], dtype=jnp.int32)[None, :]
    ).astype(jnp.float32)
    inner_sum = jnp.dot(features, w_student, preferred_element_type=jnp.float32) + jnp.dot(
        onehot, species_embed, precision=HIGHEST_PRECISION
    )
    hidden = jax.nn.silu(inner_sum)
    return (
        jnp.dot(hidden, w_charge, precision=HIGHEST_PRECISION)
        + jnp.dot(onehot, species_bias, precision=HIGHEST_PRECISION)
    ) * live_mask


def finish(
    potential, teacher_force, student_part, features, charge, live_mask, norm_gain, w_mix, w_read
):
    mean_square = jnp.mean(potential * potential, axis=1, keepdims=True)
    normed = (potential * lax.rsqrt(mean_square + 1e-06) * norm_gain[None, :]).astype(jnp.bfloat16)
    update = jax.nn.silu(jnp.dot(normed, w_mix, preferred_element_type=jnp.float32))
    combined = features.astype(jnp.float32) + update
    teacher_energy = jnp.dot(combined, w_read, precision=HIGHEST_PRECISION)
    student_energy = 0.5 * charge * student_part[:, 0]
    forces = charge[:, None] * student_part[:, 1:4]
    misfit = (student_energy - teacher_energy) ** 2 + jnp.sum(
        (forces - teacher_force) ** 2, axis=1
    ) / 3.0
    return (
        combined.astype(jnp.bfloat16),
        teacher_force,
        forces,
        student_energy,
        live_mask * misfit,
    )


def sum_over_atoms(payload):
    part = lax.psum_scatter(payload, "y", scatter_dimension=0, tiled=True)
    part = lax.psum_scatter(part, "x", scatter_dimension=0, tiled=True)
    part = lax.psum(part, "zh")
    part = lax.all_gather(part, "x", axis=0, tiled=True)
    return lax.all_gather(part, "y", axis=0, tiled=True)


def local(
    features,
    positions,
    k_indices,
    species,
    brick_counts,
    smearing,
    teacher_charge,
    norm_gain,
    w_mix,
    w_read,
    w_student,
    species_embed,
    w_charge,
    species_bias,
    student_smear,
):
    atom_rows = features.shape[0]
    k_width = k_indices.shape[1]
    channels = features.shape[1]
    atom_groups = 1
    for axis in ATOM_AXES:
        atom_groups *= lax.axis_size(axis)
    ka_groups = 1
    for axis in KA_AXES:
        ka_groups *= lax.axis_size(axis)
    inv_root = 1.0 / math.sqrt(atom_rows * atom_groups)
    live_mask = (jnp.arange(atom_rows, dtype=jnp.int32) < brick_counts[0]).astype(jnp.float32)
    masked = features * live_mask.astype(jnp.bfloat16)[:, None]
    charge = student_charge(
        features, species, live_mask, w_student, species_embed, w_charge, species_bias
    )
    charge_low = charge.astype(jnp.bfloat16)
    phases = phase_table(positions, k_indices)
    factor = lax.dot_general(
        phases, masked, (((0,), (0,)), ((), ())), preferred_element_type=jnp.float32
    )
    charge_sum = jnp.dot(charge_low, phases, preferred_element_type=jnp.float32)
    extra = jnp.concatenate(
        [
            charge_sum,
            brick_counts.astype(jnp.float32),
            jnp.zeros((PAD_ROWS * channels - 2 * k_width - 1,), jnp.float32),
        ]
    ).reshape(PAD_ROWS, channels)
    summed = sum_over_atoms(jnp.concatenate([factor, extra], axis=0))
    factor = summed[: 2 * k_width]
    extra = summed[2 * k_width :].reshape(-1)
    charge_sum = extra[: 2 * k_width]
    live_total = extra[2 * k_width]
    k_vectors, k_square = k_geometry(k_indices)
    kernel = teacher_kernel(k_square, smearing, inv_root)
    weighted = (jnp.concatenate([kernel, kernel], axis=0) * factor).astype(jnp.bfloat16)
    potential = jnp.dot(phases, weighted, preferred_element_type=jnp.float32)
    charged = (features.astype(jnp.float32) * teacher_charge[None, :]).astype(jnp.bfloat16)
    contracted = lax.dot_general(
        charged, weighted, (((1,), (1,)), ((), ())), preferred_element_type=jnp.float32
    )
    cosines = phases[:, :k_width].astype(jnp.float32)
    sines = phases[:, k_width:].astype(jnp.float32)
    force_terms = sines * contracted[:, :k_width] - cosines * contracted[:, k_width:]
    teacher_force = jnp.dot(force_terms, k_vectors.T, precision=HIGHEST_PRECISION)
    table = student_table(k_vectors, k_square, charge_sum, student_smear, inv_root, k_width)
    student_part = jnp.dot(phases, table, preferred_element_type=jnp.float32)
    packed = jnp.concatenate(
        [potential, teacher_force, student_part, jnp.zeros((atom_rows, 1), jnp.float32)], axis=1
    )
    own = lax.psum_scatter(packed, KA_AXES, scatter_dimension=0, tiled=True)
    share_rows = atom_rows // ka_groups
    ka_index = lax.axis_index(KA_AXES)
    row_start = ka_index * share_rows

    def own_rows(values):
        return lax.dynamic_slice_in_dim(values, row_start, share_rows, 0)

    teacher_features, teacher_out, forces, student_energy, misfit = finish(
        own[:, :channels],
        own[:, channels : channels + 3],
        own[:, channels + 3 : channels + 7],
        own_rows(features),
        own_rows(charge),
        own_rows(live_mask),
        norm_gain,
        w_mix,
        w_read,
    )
    loss_sum = functools.reduce(lambda v, axis: lax.psum(v, axis), ALL_AXES, jnp.sum(misfit))
    return (teacher_features, teacher_out.T, forces.T, student_energy, loss_sum / live_total)


def solution(mesh):
    sizes = dict(mesh.shape)
    ka = sizes["ka"]
    atom = sizes["atom"]
    cores = 2
    z_lo = ka // cores
    devices = mesh.devices.reshape(-1)
    y_size = 8 if atom % 8 == 0 else 1
    rest = atom // y_size
    zh = 2 if rest % 2 == 0 else 1
    x_size = rest // zh
    fine = Mesh(devices.reshape(y_size, x_size, zh, z_lo, cores), ALL_AXES)
    atom_spec = ATOM_AXES
    in_specs = (
        P(atom_spec, None),
        P(None, atom_spec),
        P(None, KA_AXES),
        P(atom_spec),
        P(atom_spec),
        P(),
        P(),
        P(),
        P(),
        P(),
        P(),
        P(),
        P(),
        P(),
        P(),
    )
    out_specs = (
        P(ALL_AXES, None),
        P(None, ALL_AXES),
        P(None, ALL_AXES),
        P(ALL_AXES),
        P(),
    )
    return jax.shard_map(local, mesh=fine, in_specs=in_specs, out_specs=out_specs, check_vma=False)
```

```python
import math

import jax
import jax.numpy as jnp
from jax import lax
from jax.sharding import Mesh
from jax.sharding import PartitionSpec as P

TWO_PI = 2.0 * math.pi
SCREEN = 20.0
HIGHEST_PRECISION = lax.Precision.HIGHEST

ATOM_AXES = ("y", "x", "zh")
KA_AXES = ("zl", "core")
ALL_AXES = ATOM_AXES + KA_AXES


def phase_table(positions, k_indices):
    k_float = k_indices.astype(jnp.float32)
    products = (
        positions[0][:, None] * k_float[0][None, :]
        + positions[1][:, None] * k_float[1][None, :]
        + positions[2][:, None] * k_float[2][None, :]
    )
    angles = TWO_PI * products
    return jnp.concatenate([jnp.cos(angles), jnp.sin(angles)], axis=1).astype(jnp.bfloat16)


def k_geometry(k_indices):
    k_vectors = TWO_PI * k_indices.astype(jnp.float32)
    k_square = (
        k_vectors[0] * k_vectors[0] + k_vectors[1] * k_vectors[1] + k_vectors[2] * k_vectors[2]
    )
    return (k_vectors, k_square)


def teacher_kernel(k_square, smearing, inv_root):
    spread = (smearing * smearing)[None, :]
    return jnp.exp(-0.5 * k_square[:, None] * spread) / (k_square[:, None] + SCREEN) * inv_root


def student_table(k_vectors, k_square, sums, student_smear, inv_root, k_width):
    spread = student_smear[0] * student_smear[0]
    kernel = jnp.exp(-0.5 * k_square * spread) / (k_square + SCREEN) * inv_root
    cos_part = kernel * sums[:k_width]
    sin_part = kernel * sums[k_width:]
    upper_rows = jnp.stack(
        [
            cos_part,
            -(k_vectors[0] * sin_part),
            -(k_vectors[1] * sin_part),
            -(k_vectors[2] * sin_part),
        ],
        axis=1,
    )
    lower_rows = jnp.stack(
        [sin_part, k_vectors[0] * cos_part, k_vectors[1] * cos_part, k_vectors[2] * cos_part],
        axis=1,
    )
    return jnp.concatenate([upper_rows, lower_rows], axis=0).astype(jnp.bfloat16)


def student_charge(features, species, live_mask, w_student, species_embed, w_charge, species_bias):
    onehot = (
        species[:, None] == jnp.arange(species_embed.shape[0], dtype=jnp.int32)[None, :]
    ).astype(jnp.float32)
    inner_sum = jnp.dot(features, w_student, preferred_element_type=jnp.float32) + jnp.dot(
        onehot, species_embed, precision=HIGHEST_PRECISION
    )
    hidden = jax.nn.silu(inner_sum)
    return (
        jnp.dot(hidden, w_charge, precision=HIGHEST_PRECISION)
        + jnp.dot(onehot, species_bias, precision=HIGHEST_PRECISION)
    ) * live_mask


def finish(
    potential, teacher_force, student_part, features, charge, live_mask, norm_gain, w_mix, w_read
):
    mean_square = jnp.mean(potential * potential, axis=1, keepdims=True)
    normed = (potential * lax.rsqrt(mean_square + 1e-06) * norm_gain[None, :]).astype(jnp.bfloat16)
    update = jax.nn.silu(jnp.dot(normed, w_mix, preferred_element_type=jnp.float32))
    combined = features.astype(jnp.float32) + update
    teacher_energy = jnp.dot(combined, w_read, precision=HIGHEST_PRECISION)
    student_energy = 0.5 * charge * student_part[:, 0]
    forces = charge[:, None] * student_part[:, 1:4]
    misfit = (student_energy - teacher_energy) ** 2 + jnp.sum(
        (forces - teacher_force) ** 2, axis=1
    ) / 3.0
    return (
        combined.astype(jnp.bfloat16),
        teacher_force,
        forces,
        student_energy,
        live_mask * misfit,
    )


def sum_over_atoms(payload):
    parts = lax.all_to_all(payload, ATOM_AXES, 0, 0, tiled=True)
    reduced = jnp.sum(parts, axis=0, keepdims=True)
    spread = jnp.broadcast_to(reduced, payload.shape)
    return lax.all_to_all(spread, ATOM_AXES, 0, 0, tiled=True)


def sum_over_ka(payload):
    parts = lax.all_to_all(payload, KA_AXES, 0, 0, tiled=True)
    return jnp.sum(parts, axis=0)


def sum_over_all(value):
    devices = 1
    for axis in ALL_AXES:
        devices *= lax.axis_size(axis)
    copies = jnp.broadcast_to(value.reshape(1), (devices,))
    return jnp.sum(lax.all_to_all(copies, ALL_AXES, 0, 0, tiled=True))


def local(
    features,
    positions,
    k_indices,
    species,
    brick_counts,
    smearing,
    teacher_charge,
    norm_gain,
    w_mix,
    w_read,
    w_student,
    species_embed,
    w_charge,
    species_bias,
    student_smear,
):
    atom_rows = features.shape[0]
    k_width = k_indices.shape[1]
    channels = features.shape[1]
    atom_groups = 1
    for axis in ATOM_AXES:
        atom_groups *= lax.axis_size(axis)
    ka_groups = 1
    for axis in KA_AXES:
        ka_groups *= lax.axis_size(axis)
    inv_root = 1.0 / math.sqrt(atom_rows * atom_groups)
    live_mask = (jnp.arange(atom_rows, dtype=jnp.int32) < brick_counts[0]).astype(jnp.float32)
    masked = features * live_mask.astype(jnp.bfloat16)[:, None]
    charge = student_charge(
        features, species, live_mask, w_student, species_embed, w_charge, species_bias
    )
    charge_low = charge.astype(jnp.bfloat16)
    phases = phase_table(positions, k_indices)
    factor = lax.dot_general(
        phases, masked, (((0,), (0,)), ((), ())), preferred_element_type=jnp.float32
    )
    charge_sum = jnp.dot(charge_low, phases, preferred_element_type=jnp.float32)
    rows_each = 2 * k_width // atom_groups
    extra = jnp.concatenate(
        [
            charge_sum,
            brick_counts.astype(jnp.float32),
            jnp.zeros((atom_groups * channels - 2 * k_width - 1,), jnp.float32),
        ]
    ).reshape(atom_groups, 1, channels)
    payload = jnp.concatenate([factor.reshape(atom_groups, rows_each, channels), extra], axis=1)
    summed = sum_over_atoms(payload)
    factor = summed[:, :rows_each].reshape(2 * k_width, channels)
    extra = summed[:, rows_each:].reshape(-1)
    charge_sum = extra[: 2 * k_width]
    live_total = extra[2 * k_width]
    k_vectors, k_square = k_geometry(k_indices)
    kernel = teacher_kernel(k_square, smearing, inv_root)
    weighted = (jnp.concatenate([kernel, kernel], axis=0) * factor).astype(jnp.bfloat16)
    potential = jnp.dot(phases, weighted, preferred_element_type=jnp.float32)
    charged = (features.astype(jnp.float32) * teacher_charge[None, :]).astype(jnp.bfloat16)
    contracted = lax.dot_general(
        charged, weighted, (((1,), (1,)), ((), ())), preferred_element_type=jnp.float32
    )
    cosines = phases[:, :k_width].astype(jnp.float32)
    sines = phases[:, k_width:].astype(jnp.float32)
    force_terms = sines * contracted[:, :k_width] - cosines * contracted[:, k_width:]
    terms_high = force_terms.astype(jnp.bfloat16)
    terms_low = (force_terms - terms_high.astype(jnp.float32)).astype(jnp.bfloat16)
    k_low = k_indices.astype(jnp.bfloat16)
    teacher_force_t = TWO_PI * (
        lax.dot_general(k_low, terms_high, (((1,), (1,)), ((), ())), preferred_element_type=jnp.float32)
        + lax.dot_general(k_low, terms_low, (((1,), (1,)), ((), ())), preferred_element_type=jnp.float32)
    )
    table = student_table(k_vectors, k_square, charge_sum, student_smear, inv_root, k_width)
    student_part_t = lax.dot_general(
        table, phases, (((0,), (1,)), ((), ())), preferred_element_type=jnp.float32
    )
    share_rows = atom_rows // ka_groups
    side = jnp.concatenate(
        [teacher_force_t, student_part_t, jnp.zeros((1, atom_rows), jnp.float32)], axis=0
    )
    side = side.reshape(8, ka_groups, share_rows).transpose(1, 0, 2)
    packed = jnp.concatenate([potential.reshape(ka_groups, share_rows, channels), side], axis=1)
    own = sum_over_ka(packed)
    ka_index = lax.axis_index(KA_AXES)
    row_start = ka_index * share_rows

    def own_rows(values):
        return lax.dynamic_slice_in_dim(values, row_start, share_rows, 0)

    own_side = own[share_rows:].T
    teacher_features, teacher_out, forces, student_energy, misfit = finish(
        own[:share_rows],
        own_side[:, 0:3],
        own_side[:, 3:7],
        own_rows(features),
        own_rows(charge),
        own_rows(live_mask),
        norm_gain,
        w_mix,
        w_read,
    )
    loss_sum = sum_over_all(jnp.sum(misfit))
    return (teacher_features, teacher_out.T, forces.T, student_energy, loss_sum / live_total)


def solution(mesh):
    sizes = dict(mesh.shape)
    ka = sizes["ka"]
    atom = sizes["atom"]
    cores = 2
    z_lo = ka // cores
    devices = mesh.devices.reshape(-1)
    y_size = 8 if atom % 8 == 0 else 1
    rest = atom // y_size
    zh = 2 if rest % 2 == 0 else 1
    x_size = rest // zh
    fine = Mesh(devices.reshape(y_size, x_size, zh, z_lo, cores), ALL_AXES)
    atom_spec = ATOM_AXES
    in_specs = (
        P(atom_spec, None),
        P(None, atom_spec),
        P(None, KA_AXES),
        P(atom_spec),
        P(atom_spec),
        P(),
        P(),
        P(),
        P(),
        P(),
        P(),
        P(),
        P(),
        P(),
        P(),
    )
    out_specs = (
        P(ALL_AXES, None),
        P(None, ALL_AXES),
        P(None, ALL_AXES),
        P(ALL_AXES),
        P(),
    )
    return jax.shard_map(local, mesh=fine, in_specs=in_specs, out_specs=out_specs, check_vma=False)
```

```python
import math

import jax
import jax.numpy as jnp
from jax import lax
from jax.sharding import Mesh
from jax.sharding import PartitionSpec as P

TWO_PI = 2.0 * math.pi
SCREEN = 20.0
HIGHEST_PRECISION = lax.Precision.HIGHEST

ATOM_AXES = ("y", "x", "zh")
KA_AXES = ("zl", "core")
ALL_AXES = ATOM_AXES + KA_AXES


def phase_table(positions, k_indices):
    k_float = k_indices.astype(jnp.float32)
    products = (
        positions[0][:, None] * k_float[0][None, :]
        + positions[1][:, None] * k_float[1][None, :]
        + positions[2][:, None] * k_float[2][None, :]
    )
    angles = TWO_PI * products
    return jnp.concatenate([jnp.cos(angles), jnp.sin(angles)], axis=1).astype(jnp.bfloat16)


def k_geometry(k_indices):
    k_vectors = TWO_PI * k_indices.astype(jnp.float32)
    k_square = (
        k_vectors[0] * k_vectors[0] + k_vectors[1] * k_vectors[1] + k_vectors[2] * k_vectors[2]
    )
    return (k_vectors, k_square)


def teacher_kernel(k_square, smearing, inv_root):
    spread = (smearing * smearing)[None, :]
    return jnp.exp(-0.5 * k_square[:, None] * spread) / (k_square[:, None] + SCREEN) * inv_root


def student_table(k_vectors, k_square, sums, student_smear, inv_root, k_width):
    spread = student_smear[0] * student_smear[0]
    kernel = jnp.exp(-0.5 * k_square * spread) / (k_square + SCREEN) * inv_root
    cos_part = kernel * sums[:k_width]
    sin_part = kernel * sums[k_width:]
    upper_rows = jnp.stack(
        [
            cos_part,
            -(k_vectors[0] * sin_part),
            -(k_vectors[1] * sin_part),
            -(k_vectors[2] * sin_part),
        ],
        axis=1,
    )
    lower_rows = jnp.stack(
        [sin_part, k_vectors[0] * cos_part, k_vectors[1] * cos_part, k_vectors[2] * cos_part],
        axis=1,
    )
    return jnp.concatenate([upper_rows, lower_rows], axis=0).astype(jnp.bfloat16)


def student_charge(features, species, live_mask, w_student, species_embed, w_charge, species_bias):
    onehot = (
        species[:, None] == jnp.arange(species_embed.shape[0], dtype=jnp.int32)[None, :]
    ).astype(jnp.float32)
    inner_sum = jnp.dot(features, w_student, preferred_element_type=jnp.float32) + jnp.dot(
        onehot, species_embed, precision=HIGHEST_PRECISION
    )
    hidden = jax.nn.silu(inner_sum)
    return (
        jnp.dot(hidden, w_charge, precision=HIGHEST_PRECISION)
        + jnp.dot(onehot, species_bias, precision=HIGHEST_PRECISION)
    ) * live_mask


def finish(
    potential, teacher_force, student_part, features, charge, live_mask, norm_gain, w_mix, w_read
):
    mean_square = jnp.mean(potential * potential, axis=1, keepdims=True)
    normed = (potential * lax.rsqrt(mean_square + 1e-06) * norm_gain[None, :]).astype(jnp.bfloat16)
    update = jax.nn.silu(jnp.dot(normed, w_mix, preferred_element_type=jnp.float32))
    combined = features.astype(jnp.float32) + update
    teacher_energy = jnp.dot(combined, w_read, precision=HIGHEST_PRECISION)
    student_energy = 0.5 * charge * student_part[:, 0]
    forces = charge[:, None] * student_part[:, 1:4]
    misfit = (student_energy - teacher_energy) ** 2 + jnp.sum(
        (forces - teacher_force) ** 2, axis=1
    ) / 3.0
    return (
        combined.astype(jnp.bfloat16),
        teacher_force,
        forces,
        student_energy,
        live_mask * misfit,
    )


def sum_over_atoms(payload):
    parts = lax.all_to_all(payload, ATOM_AXES, 0, 0, tiled=True)
    reduced = jnp.sum(parts, axis=0, keepdims=True)
    spread = jnp.broadcast_to(reduced, payload.shape)
    return lax.all_to_all(spread, ATOM_AXES, 0, 0, tiled=True)


def sum_over_ka(payload):
    parts = lax.all_to_all(payload, "core", 1, 1, tiled=True)
    chip = jnp.sum(parts, axis=1)
    parts = lax.all_to_all(chip, "zl", 0, 0, tiled=True)
    return jnp.sum(parts, axis=0)


def sum_over_all(values):
    devices = 1
    for axis in ALL_AXES:
        devices *= lax.axis_size(axis)
    copies = jnp.broadcast_to(values[None, :], (devices, values.shape[0]))
    return jnp.sum(lax.all_to_all(copies, ALL_AXES, 0, 0, tiled=True), axis=0)


def local(
    features,
    positions,
    k_indices,
    species,
    brick_counts,
    smearing,
    teacher_charge,
    norm_gain,
    w_mix,
    w_read,
    w_student,
    species_embed,
    w_charge,
    species_bias,
    student_smear,
):
    atom_rows = features.shape[0]
    k_width = k_indices.shape[1]
    channels = features.shape[1]
    atom_groups = 1
    for axis in ATOM_AXES:
        atom_groups *= lax.axis_size(axis)
    ka_groups = 1
    for axis in KA_AXES:
        ka_groups *= lax.axis_size(axis)
    inv_root = 1.0 / math.sqrt(atom_rows * atom_groups)
    live_mask = (jnp.arange(atom_rows, dtype=jnp.int32) < brick_counts[0]).astype(jnp.float32)
    masked = features * live_mask.astype(jnp.bfloat16)[:, None]
    charge = student_charge(
        features, species, live_mask, w_student, species_embed, w_charge, species_bias
    )
    charge_low = charge.astype(jnp.bfloat16)
    phases = lax.optimization_barrier(phase_table(positions, k_indices))
    factor = lax.dot_general(
        phases, masked, (((0,), (0,)), ((), ())), preferred_element_type=jnp.float32
    )
    charge_sum = jnp.dot(charge_low, phases, preferred_element_type=jnp.float32)
    rows_each = 2 * k_width // atom_groups
    lanes = 128
    factor_part = factor.reshape(atom_groups, rows_each * channels // lanes, lanes)
    charge_part = jnp.pad(
        charge_sum.reshape(atom_groups, 1, rows_each), ((0, 0), (0, 0), (0, lanes - rows_each))
    )
    summed = sum_over_atoms(jnp.concatenate([factor_part, charge_part], axis=1))
    factor = summed[:, :-1].reshape(2 * k_width, channels)
    charge_sum = summed[:, -1, :rows_each].reshape(-1)
    k_vectors, k_square = k_geometry(k_indices)
    kernel = teacher_kernel(k_square, smearing, inv_root)
    weighted = (jnp.concatenate([kernel, kernel], axis=0) * factor).astype(jnp.bfloat16)
    potential = jnp.dot(phases, weighted, preferred_element_type=jnp.float32)
    charged = (features.astype(jnp.float32) * teacher_charge[None, :]).astype(jnp.bfloat16)
    contracted = lax.dot_general(
        charged, weighted, (((1,), (1,)), ((), ())), preferred_element_type=jnp.float32
    )
    cosines = phases[:, :k_width].astype(jnp.float32)
    sines = phases[:, k_width:].astype(jnp.float32)
    force_terms = sines * contracted[:, :k_width] - cosines * contracted[:, k_width:]
    terms_high = force_terms.astype(jnp.bfloat16)
    terms_low = (force_terms - terms_high.astype(jnp.float32)).astype(jnp.bfloat16)
    k_low = k_indices.astype(jnp.bfloat16)
    teacher_force_t = TWO_PI * (
        lax.dot_general(k_low, terms_high, (((1,), (1,)), ((), ())), preferred_element_type=jnp.float32)
        + lax.dot_general(k_low, terms_low, (((1,), (1,)), ((), ())), preferred_element_type=jnp.float32)
    )
    table = student_table(k_vectors, k_square, charge_sum, student_smear, inv_root, k_width)
    student_part_t = lax.dot_general(
        table, phases, (((0,), (1,)), ((), ())), preferred_element_type=jnp.float32
    )
    share_rows = atom_rows // ka_groups
    side = jnp.concatenate(
        [teacher_force_t, student_part_t, jnp.zeros((1, atom_rows), jnp.float32)], axis=0
    )
    side = side.reshape(8, ka_groups, share_rows).transpose(1, 0, 2)
    packed = jnp.concatenate([potential.reshape(ka_groups, share_rows, channels), side], axis=1)
    z_lo = lax.axis_size("zl")
    packed = packed.reshape(z_lo, ka_groups // z_lo, share_rows + 8, channels)
    own = sum_over_ka(packed)
    ka_index = lax.axis_index(KA_AXES)
    row_start = ka_index * share_rows

    def own_rows(values):
        return lax.dynamic_slice_in_dim(values, row_start, share_rows, 0)

    own_side = own[share_rows:].T
    teacher_features, teacher_out, forces, student_energy, misfit = finish(
        own[:share_rows],
        own_side[:, 0:3],
        own_side[:, 3:7],
        own_rows(features),
        own_rows(charge),
        own_rows(live_mask),
        norm_gain,
        w_mix,
        w_read,
    )
    totals = sum_over_all(jnp.stack([jnp.sum(misfit), jnp.sum(own_rows(live_mask))]))
    return (teacher_features, teacher_out.T, forces.T, student_energy, totals[0] / totals[1])


def solution(mesh):
    sizes = dict(mesh.shape)
    ka = sizes["ka"]
    atom = sizes["atom"]
    cores = 2
    z_lo = ka // cores
    devices = mesh.devices.reshape(-1)
    y_size = 8 if atom % 8 == 0 else 1
    rest = atom // y_size
    zh = 2 if rest % 2 == 0 else 1
    x_size = rest // zh
    fine = Mesh(devices.reshape(y_size, x_size, zh, z_lo, cores), ALL_AXES)
    atom_spec = ATOM_AXES
    in_specs = (
        P(atom_spec, None),
        P(None, atom_spec),
        P(None, KA_AXES),
        P(atom_spec),
        P(atom_spec),
        P(),
        P(),
        P(),
        P(),
        P(),
        P(),
        P(),
        P(),
        P(),
        P(),
    )
    out_specs = (
        P(ALL_AXES, None),
        P(None, ALL_AXES),
        P(None, ALL_AXES),
        P(ALL_AXES),
        P(),
    )
    return jax.shard_map(local, mesh=fine, in_specs=in_specs, out_specs=out_specs, check_vma=False)
```

```python
import math

import jax
import jax.numpy as jnp
from jax import lax
from jax.sharding import Mesh
from jax.sharding import PartitionSpec as P

TWO_PI = 2.0 * math.pi
SCREEN = 20.0
HIGHEST_PRECISION = lax.Precision.HIGHEST

ATOM_AXES = ("y", "x", "zh")
KA_AXES = ("zl", "core")
ALL_AXES = ATOM_AXES + KA_AXES


def phase_table(positions, k_indices):
    k_float = k_indices.astype(jnp.float32)
    products = (
        positions[0][:, None] * k_float[0][None, :]
        + positions[1][:, None] * k_float[1][None, :]
        + positions[2][:, None] * k_float[2][None, :]
    )
    angles = TWO_PI * products
    return jnp.concatenate([jnp.cos(angles), jnp.sin(angles)], axis=1).astype(jnp.bfloat16)


def k_geometry(k_indices):
    k_vectors = TWO_PI * k_indices.astype(jnp.float32)
    k_square = (
        k_vectors[0] * k_vectors[0] + k_vectors[1] * k_vectors[1] + k_vectors[2] * k_vectors[2]
    )
    return (k_vectors, k_square)


def teacher_kernel(k_square, smearing, inv_root):
    spread = (smearing * smearing)[None, :]
    return jnp.exp(-0.5 * k_square[:, None] * spread) / (k_square[:, None] + SCREEN) * inv_root


def student_table(k_vectors, k_square, sums, student_smear, inv_root, k_width):
    spread = student_smear[0] * student_smear[0]
    kernel = jnp.exp(-0.5 * k_square * spread) / (k_square + SCREEN) * inv_root
    cos_part = kernel * sums[:k_width]
    sin_part = kernel * sums[k_width:]
    upper_rows = jnp.stack(
        [
            cos_part,
            -(k_vectors[0] * sin_part),
            -(k_vectors[1] * sin_part),
            -(k_vectors[2] * sin_part),
        ],
        axis=1,
    )
    lower_rows = jnp.stack(
        [sin_part, k_vectors[0] * cos_part, k_vectors[1] * cos_part, k_vectors[2] * cos_part],
        axis=1,
    )
    return jnp.concatenate([upper_rows, lower_rows], axis=0).astype(jnp.bfloat16)


def student_charge(features, species, live_mask, w_student, species_embed, w_charge, species_bias):
    onehot = (
        species[:, None] == jnp.arange(species_embed.shape[0], dtype=jnp.int32)[None, :]
    ).astype(jnp.float32)
    inner_sum = jnp.dot(features, w_student, preferred_element_type=jnp.float32) + jnp.dot(
        onehot, species_embed, precision=HIGHEST_PRECISION
    )
    hidden = jax.nn.silu(inner_sum)
    return (
        jnp.dot(hidden, w_charge, precision=HIGHEST_PRECISION)
        + jnp.dot(onehot, species_bias, precision=HIGHEST_PRECISION)
    ) * live_mask


def finish(
    potential, teacher_force, student_part, features, charge, live_mask, norm_gain, w_mix, w_read
):
    mean_square = jnp.mean(potential * potential, axis=1, keepdims=True)
    normed = (potential * lax.rsqrt(mean_square + 1e-06) * norm_gain[None, :]).astype(jnp.bfloat16)
    update = jax.nn.silu(jnp.dot(normed, w_mix, preferred_element_type=jnp.float32))
    combined = features.astype(jnp.float32) + update
    teacher_energy = jnp.dot(combined, w_read, precision=HIGHEST_PRECISION)
    student_energy = 0.5 * charge * student_part[:, 0]
    forces = charge[:, None] * student_part[:, 1:4]
    misfit = (student_energy - teacher_energy) ** 2 + jnp.sum(
        (forces - teacher_force) ** 2, axis=1
    ) / 3.0
    return (
        combined.astype(jnp.bfloat16),
        teacher_force,
        forces,
        student_energy,
        live_mask * misfit,
    )


def sum_over_atoms(payload):
    parts = lax.all_to_all(payload, ATOM_AXES, 0, 0, tiled=True)
    reduced = jnp.sum(parts, axis=0, keepdims=True)
    spread = jnp.broadcast_to(reduced, payload.shape)
    return lax.all_to_all(spread, ATOM_AXES, 0, 0, tiled=True)


def sum_over_ka(payload):
    parts = lax.all_to_all(payload, "core", 1, 1, tiled=True)
    chip = jnp.sum(parts, axis=1)
    parts = lax.all_to_all(chip, "zl", 0, 0, tiled=True)
    return jnp.sum(parts, axis=0)


def sum_over_all(values):
    devices = 1
    for axis in ALL_AXES:
        devices *= lax.axis_size(axis)
    copies = jnp.broadcast_to(values[None, :], (devices, values.shape[0]))
    return jnp.sum(lax.all_to_all(copies, ALL_AXES, 0, 0, tiled=True), axis=0)


def local(
    features,
    positions,
    k_indices,
    species,
    brick_counts,
    smearing,
    teacher_charge,
    norm_gain,
    w_mix,
    w_read,
    w_student,
    species_embed,
    w_charge,
    species_bias,
    student_smear,
):
    atom_rows = features.shape[0]
    k_width = k_indices.shape[1]
    channels = features.shape[1]
    atom_groups = 1
    for axis in ATOM_AXES:
        atom_groups *= lax.axis_size(axis)
    ka_groups = 1
    for axis in KA_AXES:
        ka_groups *= lax.axis_size(axis)
    inv_root = 1.0 / math.sqrt(atom_rows * atom_groups)
    live_mask = (jnp.arange(atom_rows, dtype=jnp.int32) < brick_counts[0]).astype(jnp.float32)
    masked = features * live_mask.astype(jnp.bfloat16)[:, None]
    charge = student_charge(
        features, species, live_mask, w_student, species_embed, w_charge, species_bias
    )
    charge_low = charge.astype(jnp.bfloat16)
    phases = lax.optimization_barrier(phase_table(positions, k_indices))
    factor = lax.dot_general(
        phases, masked, (((0,), (0,)), ((), ())), preferred_element_type=jnp.float32
    )
    charge_sum = jnp.dot(charge_low, phases, preferred_element_type=jnp.float32)
    rows_each = 2 * k_width // atom_groups
    flat = rows_each * channels
    payload = jnp.concatenate(
        [factor.reshape(atom_groups, flat), charge_sum.reshape(atom_groups, rows_each)], axis=1
    )
    summed = sum_over_atoms(payload)
    factor = summed[:, :flat].reshape(2 * k_width, channels)
    charge_sum = summed[:, flat:].reshape(-1)
    k_vectors, k_square = k_geometry(k_indices)
    kernel = teacher_kernel(k_square, smearing, inv_root)
    weighted = (jnp.concatenate([kernel, kernel], axis=0) * factor).astype(jnp.bfloat16)
    potential = jnp.dot(phases, weighted, preferred_element_type=jnp.float32)
    charged = (features.astype(jnp.float32) * teacher_charge[None, :]).astype(jnp.bfloat16)
    contracted = lax.dot_general(
        charged, weighted, (((1,), (1,)), ((), ())), preferred_element_type=jnp.float32
    )
    cosines = phases[:, :k_width].astype(jnp.float32)
    sines = phases[:, k_width:].astype(jnp.float32)
    force_terms = sines * contracted[:, :k_width] - cosines * contracted[:, k_width:]
    terms_high = force_terms.astype(jnp.bfloat16)
    terms_low = (force_terms - terms_high.astype(jnp.float32)).astype(jnp.bfloat16)
    k_low = k_indices.astype(jnp.bfloat16)
    teacher_force_t = TWO_PI * (
        lax.dot_general(k_low, terms_high, (((1,), (1,)), ((), ())), preferred_element_type=jnp.float32)
        + lax.dot_general(k_low, terms_low, (((1,), (1,)), ((), ())), preferred_element_type=jnp.float32)
    )
    table = student_table(k_vectors, k_square, charge_sum, student_smear, inv_root, k_width)
    student_part_t = lax.dot_general(
        table, phases, (((0,), (1,)), ((), ())), preferred_element_type=jnp.float32
    )
    share_rows = atom_rows // ka_groups
    side = jnp.concatenate(
        [teacher_force_t, student_part_t, jnp.zeros((1, atom_rows), jnp.float32)], axis=0
    )
    side = side.reshape(8, ka_groups, share_rows).transpose(1, 0, 2)
    packed = jnp.concatenate([potential.reshape(ka_groups, share_rows, channels), side], axis=1)
    z_lo = lax.axis_size("zl")
    packed = packed.reshape(z_lo, ka_groups // z_lo, share_rows + 8, channels)
    own = sum_over_ka(packed)
    ka_index = lax.axis_index(KA_AXES)
    row_start = ka_index * share_rows

    def own_rows(values):
        return lax.dynamic_slice_in_dim(values, row_start, share_rows, 0)

    own_side = own[share_rows:].T
    teacher_features, teacher_out, forces, student_energy, misfit = finish(
        own[:share_rows],
        own_side[:, 0:3],
        own_side[:, 3:7],
        own_rows(features),
        own_rows(charge),
        own_rows(live_mask),
        norm_gain,
        w_mix,
        w_read,
    )
    totals = sum_over_all(jnp.stack([jnp.sum(misfit), jnp.sum(own_rows(live_mask))]))
    return (teacher_features, teacher_out.T, forces.T, student_energy, totals[0] / totals[1])


def solution(mesh):
    sizes = dict(mesh.shape)
    ka = sizes["ka"]
    atom = sizes["atom"]
    cores = 2
    z_lo = ka // cores
    devices = mesh.devices.reshape(-1)
    y_size = 8 if atom % 8 == 0 else 1
    rest = atom // y_size
    zh = 2 if rest % 2 == 0 else 1
    x_size = rest // zh
    fine = Mesh(devices.reshape(y_size, x_size, zh, z_lo, cores), ALL_AXES)
    atom_spec = ATOM_AXES
    in_specs = (
        P(atom_spec, None),
        P(None, atom_spec),
        P(None, KA_AXES),
        P(atom_spec),
        P(atom_spec),
        P(),
        P(),
        P(),
        P(),
        P(),
        P(),
        P(),
        P(),
        P(),
        P(),
    )
    out_specs = (
        P(ALL_AXES, None),
        P(None, ALL_AXES),
        P(None, ALL_AXES),
        P(ALL_AXES),
        P(),
    )
    return jax.shard_map(local, mesh=fine, in_specs=in_specs, out_specs=out_specs, check_vma=False)
```

```python
import math

import jax
import jax.numpy as jnp
from jax import lax
from jax.sharding import Mesh
from jax.sharding import PartitionSpec as P

TWO_PI = 2.0 * math.pi
SCREEN = 20.0
HIGHEST_PRECISION = lax.Precision.HIGHEST

ATOM_AXES = ("y", "x", "zh")
KA_AXES = ("zl", "core")
ALL_AXES = ATOM_AXES + KA_AXES


def phase_table(positions, k_indices):
    k_float = k_indices.astype(jnp.float32)
    products = (
        positions[0][:, None] * k_float[0][None, :]
        + positions[1][:, None] * k_float[1][None, :]
        + positions[2][:, None] * k_float[2][None, :]
    )
    angles = TWO_PI * products
    return jnp.concatenate([jnp.cos(angles), jnp.sin(angles)], axis=1).astype(jnp.bfloat16)


def k_geometry(k_indices):
    k_vectors = TWO_PI * k_indices.astype(jnp.float32)
    k_square = (
        k_vectors[0] * k_vectors[0] + k_vectors[1] * k_vectors[1] + k_vectors[2] * k_vectors[2]
    )
    return (k_vectors, k_square)


def teacher_kernel(k_square, smearing, inv_root):
    spread = (smearing * smearing)[None, :]
    return jnp.exp(-0.5 * k_square[:, None] * spread) / (k_square[:, None] + SCREEN) * inv_root


def student_table(k_vectors, k_square, sums, student_smear, inv_root, k_width):
    spread = student_smear[0] * student_smear[0]
    kernel = jnp.exp(-0.5 * k_square * spread) / (k_square + SCREEN) * inv_root
    cos_part = kernel * sums[:k_width]
    sin_part = kernel * sums[k_width:]
    upper_rows = jnp.stack(
        [
            cos_part,
            -(k_vectors[0] * sin_part),
            -(k_vectors[1] * sin_part),
            -(k_vectors[2] * sin_part),
        ],
        axis=1,
    )
    lower_rows = jnp.stack(
        [sin_part, k_vectors[0] * cos_part, k_vectors[1] * cos_part, k_vectors[2] * cos_part],
        axis=1,
    )
    return jnp.concatenate([upper_rows, lower_rows], axis=0).astype(jnp.bfloat16)


def student_charge(features, species, live_mask, w_student, species_embed, w_charge, species_bias):
    onehot = (
        species[:, None] == jnp.arange(species_embed.shape[0], dtype=jnp.int32)[None, :]
    ).astype(jnp.float32)
    inner_sum = jnp.dot(features, w_student, preferred_element_type=jnp.float32) + jnp.dot(
        onehot, species_embed, precision=HIGHEST_PRECISION
    )
    hidden = jax.nn.silu(inner_sum)
    return (
        jnp.dot(hidden, w_charge, precision=HIGHEST_PRECISION)
        + jnp.dot(onehot, species_bias, precision=HIGHEST_PRECISION)
    ) * live_mask


def finish(
    potential, teacher_force, student_part, features, charge, live_mask, norm_gain, w_mix, w_read
):
    mean_square = jnp.mean(potential * potential, axis=1, keepdims=True)
    normed = (potential * lax.rsqrt(mean_square + 1e-06) * norm_gain[None, :]).astype(jnp.bfloat16)
    update = jax.nn.silu(jnp.dot(normed, w_mix, preferred_element_type=jnp.float32))
    combined = features.astype(jnp.float32) + update
    teacher_energy = jnp.dot(combined, w_read, precision=HIGHEST_PRECISION)
    student_energy = 0.5 * charge * student_part[:, 0]
    forces = charge[:, None] * student_part[:, 1:4]
    misfit = (student_energy - teacher_energy) ** 2 + jnp.sum(
        (forces - teacher_force) ** 2, axis=1
    ) / 3.0
    return (
        combined.astype(jnp.bfloat16),
        teacher_force,
        forces,
        student_energy,
        live_mask * misfit,
    )


def sum_over_atoms(payload):
    parts = lax.all_to_all(payload, ATOM_AXES, 0, 0, tiled=True)
    reduced = jnp.sum(parts, axis=0, keepdims=True)
    spread = jnp.broadcast_to(reduced, payload.shape)
    return lax.all_to_all(spread, ATOM_AXES, 0, 0, tiled=True)


def sum_over_ka(payload):
    parts = lax.all_to_all(payload, "core", 1, 1, tiled=True)
    chip = jnp.sum(parts, axis=1)
    parts = lax.all_to_all(chip, "zl", 0, 0, tiled=True)
    return jnp.sum(parts, axis=0)


def sum_over_all(values):
    pair = jnp.broadcast_to(values[None, :], (lax.axis_size("core"), values.shape[0]))
    chip = jnp.sum(lax.all_to_all(pair, "core", 0, 0, tiled=True), axis=0)
    chips = 1
    for axis in ALL_AXES[:-1]:
        chips *= lax.axis_size(axis)
    copies = jnp.broadcast_to(chip[None, :], (chips, values.shape[0]))
    return jnp.sum(lax.all_to_all(copies, ALL_AXES[:-1], 0, 0, tiled=True), axis=0)


def local(
    features,
    positions,
    k_indices,
    species,
    brick_counts,
    smearing,
    teacher_charge,
    norm_gain,
    w_mix,
    w_read,
    w_student,
    species_embed,
    w_charge,
    species_bias,
    student_smear,
):
    atom_rows = features.shape[0]
    k_width = k_indices.shape[1]
    channels = features.shape[1]
    atom_groups = 1
    for axis in ATOM_AXES:
        atom_groups *= lax.axis_size(axis)
    ka_groups = 1
    for axis in KA_AXES:
        ka_groups *= lax.axis_size(axis)
    inv_root = 1.0 / math.sqrt(atom_rows * atom_groups)
    live_mask = (jnp.arange(atom_rows, dtype=jnp.int32) < brick_counts[0]).astype(jnp.float32)
    masked = features * live_mask.astype(jnp.bfloat16)[:, None]
    charge = student_charge(
        features, species, live_mask, w_student, species_embed, w_charge, species_bias
    )
    charge_low = charge.astype(jnp.bfloat16)
    phases = lax.optimization_barrier(phase_table(positions, k_indices))
    factor = lax.dot_general(
        phases, masked, (((0,), (0,)), ((), ())), preferred_element_type=jnp.float32
    )
    charge_sum = jnp.dot(charge_low, phases, preferred_element_type=jnp.float32)
    rows_each = 2 * k_width // atom_groups
    flat = rows_each * channels
    payload = jnp.concatenate(
        [factor.reshape(atom_groups, flat), charge_sum.reshape(atom_groups, rows_each)], axis=1
    )
    summed = sum_over_atoms(payload)
    factor = summed[:, :flat].reshape(2 * k_width, channels)
    charge_sum = summed[:, flat:].reshape(-1)
    k_vectors, k_square = k_geometry(k_indices)
    kernel = teacher_kernel(k_square, smearing, inv_root)
    weighted = (jnp.concatenate([kernel, kernel], axis=0) * factor).astype(jnp.bfloat16)
    potential = jnp.dot(phases, weighted, preferred_element_type=jnp.float32)
    charged = (features.astype(jnp.float32) * teacher_charge[None, :]).astype(jnp.bfloat16)
    contracted = lax.dot_general(
        charged, weighted, (((1,), (1,)), ((), ())), preferred_element_type=jnp.float32
    )
    cosines = phases[:, :k_width].astype(jnp.float32)
    sines = phases[:, k_width:].astype(jnp.float32)
    force_terms = sines * contracted[:, :k_width] - cosines * contracted[:, k_width:]
    terms_high = force_terms.astype(jnp.bfloat16)
    terms_low = (force_terms - terms_high.astype(jnp.float32)).astype(jnp.bfloat16)
    k_low = k_indices.astype(jnp.bfloat16)
    teacher_force_t = TWO_PI * (
        lax.dot_general(k_low, terms_high, (((1,), (1,)), ((), ())), preferred_element_type=jnp.float32)
        + lax.dot_general(k_low, terms_low, (((1,), (1,)), ((), ())), preferred_element_type=jnp.float32)
    )
    table = student_table(k_vectors, k_square, charge_sum, student_smear, inv_root, k_width)
    student_part_t = lax.dot_general(
        table, phases, (((0,), (1,)), ((), ())), preferred_element_type=jnp.float32
    )
    share_rows = atom_rows // ka_groups
    side = jnp.concatenate(
        [teacher_force_t, student_part_t, jnp.zeros((1, atom_rows), jnp.float32)], axis=0
    )
    side = side.reshape(8, ka_groups, share_rows).transpose(1, 0, 2)
    packed = jnp.concatenate([potential.reshape(ka_groups, share_rows, channels), side], axis=1)
    z_lo = lax.axis_size("zl")
    packed = packed.reshape(z_lo, ka_groups // z_lo, share_rows + 8, channels)
    own = sum_over_ka(packed)
    ka_index = lax.axis_index(KA_AXES)
    row_start = ka_index * share_rows

    def own_rows(values):
        return lax.dynamic_slice_in_dim(values, row_start, share_rows, 0)

    own_side = own[share_rows:].T
    teacher_features, teacher_out, forces, student_energy, misfit = finish(
        own[:share_rows],
        own_side[:, 0:3],
        own_side[:, 3:7],
        own_rows(features),
        own_rows(charge),
        own_rows(live_mask),
        norm_gain,
        w_mix,
        w_read,
    )
    totals = sum_over_all(jnp.stack([jnp.sum(misfit), jnp.sum(own_rows(live_mask))]))
    return (teacher_features, teacher_out.T, forces.T, student_energy, totals[0] / totals[1])


def solution(mesh):
    sizes = dict(mesh.shape)
    ka = sizes["ka"]
    atom = sizes["atom"]
    cores = 2
    z_lo = ka // cores
    devices = mesh.devices.reshape(-1)
    y_size = 8 if atom % 8 == 0 else 1
    rest = atom // y_size
    zh = 2 if rest % 2 == 0 else 1
    x_size = rest // zh
    fine = Mesh(devices.reshape(y_size, x_size, zh, z_lo, cores), ALL_AXES)
    atom_spec = ATOM_AXES
    in_specs = (
        P(atom_spec, None),
        P(None, atom_spec),
        P(None, KA_AXES),
        P(atom_spec),
        P(atom_spec),
        P(),
        P(),
        P(),
        P(),
        P(),
        P(),
        P(),
        P(),
        P(),
        P(),
    )
    out_specs = (
        P(ALL_AXES, None),
        P(None, ALL_AXES),
        P(None, ALL_AXES),
        P(ALL_AXES),
        P(),
    )
    return jax.shard_map(local, mesh=fine, in_specs=in_specs, out_specs=out_specs, check_vma=False)
```

```python
import math

import jax
import jax.numpy as jnp
from jax import lax
from jax.sharding import Mesh
from jax.sharding import PartitionSpec as P

TWO_PI = 2.0 * math.pi
SCREEN = 20.0
HIGHEST_PRECISION = lax.Precision.HIGHEST

ATOM_AXES = ("y", "x", "zh")
KA_AXES = ("zl", "core")
ALL_AXES = ATOM_AXES + KA_AXES


def phase_table(positions, k_indices):
    k_float = k_indices.astype(jnp.float32)
    products = (
        positions[0][:, None] * k_float[0][None, :]
        + positions[1][:, None] * k_float[1][None, :]
        + positions[2][:, None] * k_float[2][None, :]
    )
    quarters = 4.0 * products
    quarter = jnp.round(quarters)
    angle = (quarters - quarter) * (0.5 * math.pi)
    square = angle * angle
    sine = angle * (
        1.0
        + square
        * (
            -1.0 / 6.0
            + square * (1.0 / 120.0 + square * (-1.0 / 5040.0 + square * (1.0 / 362880.0)))
        )
    )
    cosine = 1.0 + square * (
        -0.5 + square * (1.0 / 24.0 + square * (-1.0 / 720.0 + square * (1.0 / 40320.0)))
    )
    turn = quarter - 4.0 * jnp.floor(quarter * 0.25)
    odd = (turn == 1.0) | (turn == 3.0)
    cos_base = jnp.where(odd, sine, cosine)
    sin_base = jnp.where(odd, cosine, sine)
    cos_value = jnp.where((turn == 1.0) | (turn == 2.0), -cos_base, cos_base)
    sin_value = jnp.where(turn >= 2.0, -sin_base, sin_base)
    return jnp.concatenate([cos_value, sin_value], axis=1).astype(jnp.bfloat16)


def k_geometry(k_indices):
    k_vectors = TWO_PI * k_indices.astype(jnp.float32)
    k_square = (
        k_vectors[0] * k_vectors[0] + k_vectors[1] * k_vectors[1] + k_vectors[2] * k_vectors[2]
    )
    return (k_vectors, k_square)


def teacher_kernel(k_square, smearing, inv_root):
    spread = (smearing * smearing)[None, :]
    return jnp.exp(-0.5 * k_square[:, None] * spread) / (k_square[:, None] + SCREEN) * inv_root


def student_table(k_vectors, k_square, sums, student_smear, inv_root, k_width):
    spread = student_smear[0] * student_smear[0]
    kernel = jnp.exp(-0.5 * k_square * spread) / (k_square + SCREEN) * inv_root
    cos_part = kernel * sums[:k_width]
    sin_part = kernel * sums[k_width:]
    upper_rows = jnp.stack(
        [
            cos_part,
            -(k_vectors[0] * sin_part),
            -(k_vectors[1] * sin_part),
            -(k_vectors[2] * sin_part),
        ],
        axis=1,
    )
    lower_rows = jnp.stack(
        [sin_part, k_vectors[0] * cos_part, k_vectors[1] * cos_part, k_vectors[2] * cos_part],
        axis=1,
    )
    return jnp.concatenate([upper_rows, lower_rows], axis=0).astype(jnp.bfloat16)


def student_charge(features, species, live_mask, w_student, species_embed, w_charge, species_bias):
    onehot = (
        species[:, None] == jnp.arange(species_embed.shape[0], dtype=jnp.int32)[None, :]
    ).astype(jnp.float32)
    inner_sum = jnp.dot(features, w_student, preferred_element_type=jnp.float32) + jnp.dot(
        onehot, species_embed, precision=HIGHEST_PRECISION
    )
    hidden = jax.nn.silu(inner_sum)
    return (
        jnp.dot(hidden, w_charge, precision=HIGHEST_PRECISION)
        + jnp.dot(onehot, species_bias, precision=HIGHEST_PRECISION)
    ) * live_mask


def finish(
    potential, teacher_force, student_part, features, charge, live_mask, norm_gain, w_mix, w_read
):
    mean_square = jnp.mean(potential * potential, axis=1, keepdims=True)
    normed = (potential * lax.rsqrt(mean_square + 1e-06) * norm_gain[None, :]).astype(jnp.bfloat16)
    update = jax.nn.silu(jnp.dot(normed, w_mix, preferred_element_type=jnp.float32))
    combined = features.astype(jnp.float32) + update
    teacher_energy = jnp.dot(combined, w_read, precision=HIGHEST_PRECISION)
    student_energy = 0.5 * charge * student_part[:, 0]
    forces = charge[:, None] * student_part[:, 1:4]
    misfit = (student_energy - teacher_energy) ** 2 + jnp.sum(
        (forces - teacher_force) ** 2, axis=1
    ) / 3.0
    return (
        combined.astype(jnp.bfloat16),
        teacher_force,
        forces,
        student_energy,
        live_mask * misfit,
    )


def sum_over_atoms(payload):
    parts = lax.all_to_all(payload, ATOM_AXES, 0, 0, tiled=True)
    reduced = jnp.sum(parts, axis=0, keepdims=True)
    spread = jnp.broadcast_to(reduced, payload.shape)
    return lax.all_to_all(spread, ATOM_AXES, 0, 0, tiled=True)


def sum_over_ka(payload):
    parts = lax.all_to_all(payload, "core", 1, 1, tiled=True)
    chip = jnp.sum(parts, axis=1)
    parts = lax.all_to_all(chip, "zl", 0, 0, tiled=True)
    return jnp.sum(parts, axis=0)


def sum_over_all(values):
    pair = jnp.broadcast_to(values[None, :], (lax.axis_size("core"), values.shape[0]))
    chip = jnp.sum(lax.all_to_all(pair, "core", 0, 0, tiled=True), axis=0)
    chips = 1
    for axis in ALL_AXES[:-1]:
        chips *= lax.axis_size(axis)
    copies = jnp.broadcast_to(chip[None, :], (chips, values.shape[0]))
    return jnp.sum(lax.all_to_all(copies, ALL_AXES[:-1], 0, 0, tiled=True), axis=0)


def local(
    features,
    positions,
    k_indices,
    species,
    brick_counts,
    smearing,
    teacher_charge,
    norm_gain,
    w_mix,
    w_read,
    w_student,
    species_embed,
    w_charge,
    species_bias,
    student_smear,
):
    atom_rows = features.shape[0]
    k_width = k_indices.shape[1]
    channels = features.shape[1]
    atom_groups = 1
    for axis in ATOM_AXES:
        atom_groups *= lax.axis_size(axis)
    ka_groups = 1
    for axis in KA_AXES:
        ka_groups *= lax.axis_size(axis)
    inv_root = 1.0 / math.sqrt(atom_rows * atom_groups)
    live_mask = (jnp.arange(atom_rows, dtype=jnp.int32) < brick_counts[0]).astype(jnp.float32)
    masked = features * live_mask.astype(jnp.bfloat16)[:, None]
    charge = student_charge(
        features, species, live_mask, w_student, species_embed, w_charge, species_bias
    )
    charge_low = charge.astype(jnp.bfloat16)
    phases = lax.optimization_barrier(phase_table(positions, k_indices))
    factor = lax.dot_general(
        phases, masked, (((0,), (0,)), ((), ())), preferred_element_type=jnp.float32
    )
    charge_sum = jnp.dot(charge_low, phases, preferred_element_type=jnp.float32)
    rows_each = 2 * k_width // atom_groups
    flat = rows_each * channels
    payload = jnp.concatenate(
        [factor.reshape(atom_groups, flat), charge_sum.reshape(atom_groups, rows_each)], axis=1
    )
    summed = sum_over_atoms(payload)
    factor = summed[:, :flat].reshape(2 * k_width, channels)
    charge_sum = summed[:, flat:].reshape(-1)
    k_vectors, k_square = k_geometry(k_indices)
    kernel = teacher_kernel(k_square, smearing, inv_root)
    weighted = (jnp.concatenate([kernel, kernel], axis=0) * factor).astype(jnp.bfloat16)
    potential = jnp.dot(phases, weighted, preferred_element_type=jnp.float32)
    charged = (features.astype(jnp.float32) * teacher_charge[None, :]).astype(jnp.bfloat16)
    contracted = lax.dot_general(
        charged, weighted, (((1,), (1,)), ((), ())), preferred_element_type=jnp.float32
    )
    cosines = phases[:, :k_width].astype(jnp.float32)
    sines = phases[:, k_width:].astype(jnp.float32)
    force_terms = sines * contracted[:, :k_width] - cosines * contracted[:, k_width:]
    terms_high = force_terms.astype(jnp.bfloat16)
    terms_low = (force_terms - terms_high.astype(jnp.float32)).astype(jnp.bfloat16)
    k_low = k_indices.astype(jnp.bfloat16)
    teacher_force_t = TWO_PI * (
        lax.dot_general(k_low, terms_high, (((1,), (1,)), ((), ())), preferred_element_type=jnp.float32)
        + lax.dot_general(k_low, terms_low, (((1,), (1,)), ((), ())), preferred_element_type=jnp.float32)
    )
    table = student_table(k_vectors, k_square, charge_sum, student_smear, inv_root, k_width)
    student_part_t = lax.dot_general(
        table, phases, (((0,), (1,)), ((), ())), preferred_element_type=jnp.float32
    )
    share_rows = atom_rows // ka_groups
    side = jnp.concatenate(
        [teacher_force_t, student_part_t, jnp.zeros((1, atom_rows), jnp.float32)], axis=0
    )
    side = side.reshape(8, ka_groups, share_rows).transpose(1, 0, 2)
    packed = jnp.concatenate([potential.reshape(ka_groups, share_rows, channels), side], axis=1)
    z_lo = lax.axis_size("zl")
    packed = packed.reshape(z_lo, ka_groups // z_lo, share_rows + 8, channels)
    own = sum_over_ka(packed)
    ka_index = lax.axis_index(KA_AXES)
    row_start = ka_index * share_rows

    def own_rows(values):
        return lax.dynamic_slice_in_dim(values, row_start, share_rows, 0)

    own_side = own[share_rows:].T
    teacher_features, teacher_out, forces, student_energy, misfit = finish(
        own[:share_rows],
        own_side[:, 0:3],
        own_side[:, 3:7],
        own_rows(features),
        own_rows(charge),
        own_rows(live_mask),
        norm_gain,
        w_mix,
        w_read,
    )
    totals = sum_over_all(jnp.stack([jnp.sum(misfit), jnp.sum(own_rows(live_mask))]))
    return (teacher_features, teacher_out.T, forces.T, student_energy, totals[0] / totals[1])


def solution(mesh):
    sizes = dict(mesh.shape)
    ka = sizes["ka"]
    atom = sizes["atom"]
    cores = 2
    z_lo = ka // cores
    devices = mesh.devices.reshape(-1)
    y_size = 8 if atom % 8 == 0 else 1
    rest = atom // y_size
    zh = 2 if rest % 2 == 0 else 1
    x_size = rest // zh
    fine = Mesh(devices.reshape(y_size, x_size, zh, z_lo, cores), ALL_AXES)
    atom_spec = ATOM_AXES
    in_specs = (
        P(atom_spec, None),
        P(None, atom_spec),
        P(None, KA_AXES),
        P(atom_spec),
        P(atom_spec),
        P(),
        P(),
        P(),
        P(),
        P(),
        P(),
        P(),
        P(),
        P(),
        P(),
    )
    out_specs = (
        P(ALL_AXES, None),
        P(None, ALL_AXES),
        P(None, ALL_AXES),
        P(ALL_AXES),
        P(),
    )
    return jax.shard_map(local, mesh=fine, in_specs=in_specs, out_specs=out_specs, check_vma=False)
```

```python
import math

import jax
import jax.numpy as jnp
from jax import lax
from jax.sharding import Mesh
from jax.sharding import PartitionSpec as P

TWO_PI = 2.0 * math.pi
SCREEN = 20.0
HIGHEST_PRECISION = lax.Precision.HIGHEST

ATOM_AXES = ("y", "x", "zh")
KA_AXES = ("zl", "core")
ALL_AXES = ATOM_AXES + KA_AXES


def phase_table(positions, k_indices):
    k_float = k_indices.astype(jnp.float32)
    products = (
        positions[0][:, None] * k_float[0][None, :]
        + positions[1][:, None] * k_float[1][None, :]
        + positions[2][:, None] * k_float[2][None, :]
    )
    quarters = 4.0 * products
    quarter = jnp.round(quarters)
    angle = (quarters - quarter) * (0.5 * math.pi)
    square = angle * angle
    sine = angle * (
        1.0
        + square
        * (
            -1.0 / 6.0
            + square * (1.0 / 120.0 + square * (-1.0 / 5040.0 + square * (1.0 / 362880.0)))
        )
    )
    cosine = 1.0 + square * (
        -0.5 + square * (1.0 / 24.0 + square * (-1.0 / 720.0 + square * (1.0 / 40320.0)))
    )
    turn = quarter - 4.0 * jnp.floor(quarter * 0.25)
    odd = (turn == 1.0) | (turn == 3.0)
    cos_base = jnp.where(odd, sine, cosine)
    sin_base = jnp.where(odd, cosine, sine)
    cos_value = jnp.where((turn == 1.0) | (turn == 2.0), -cos_base, cos_base)
    sin_value = jnp.where(turn >= 2.0, -sin_base, sin_base)
    return jnp.concatenate([cos_value, sin_value], axis=1).astype(jnp.bfloat16)


def k_geometry(k_indices):
    k_vectors = TWO_PI * k_indices.astype(jnp.float32)
    k_square = (
        k_vectors[0] * k_vectors[0] + k_vectors[1] * k_vectors[1] + k_vectors[2] * k_vectors[2]
    )
    return (k_vectors, k_square)


def teacher_kernel(k_square, smearing, inv_root):
    spread = (smearing * smearing)[None, :]
    return jnp.exp(-0.5 * k_square[:, None] * spread) / (k_square[:, None] + SCREEN) * inv_root


def student_table(k_vectors, k_square, sums, student_smear, inv_root, k_width):
    spread = student_smear[0] * student_smear[0]
    kernel = jnp.exp(-0.5 * k_square * spread) / (k_square + SCREEN) * inv_root
    cos_part = kernel * sums[:k_width]
    sin_part = kernel * sums[k_width:]
    upper_rows = jnp.stack(
        [
            cos_part,
            -(k_vectors[0] * sin_part),
            -(k_vectors[1] * sin_part),
            -(k_vectors[2] * sin_part),
        ],
        axis=1,
    )
    lower_rows = jnp.stack(
        [sin_part, k_vectors[0] * cos_part, k_vectors[1] * cos_part, k_vectors[2] * cos_part],
        axis=1,
    )
    return jnp.concatenate([upper_rows, lower_rows], axis=0).astype(jnp.bfloat16)


def student_charge(features, species, live_mask, w_student, species_embed, w_charge, species_bias):
    onehot = (
        species[:, None] == jnp.arange(species_embed.shape[0], dtype=jnp.int32)[None, :]
    ).astype(jnp.float32)
    inner_sum = jnp.dot(features, w_student, preferred_element_type=jnp.float32) + jnp.dot(
        onehot, species_embed, precision=HIGHEST_PRECISION
    )
    hidden = jax.nn.silu(inner_sum)
    return (
        jnp.dot(hidden, w_charge, precision=HIGHEST_PRECISION)
        + jnp.dot(onehot, species_bias, precision=HIGHEST_PRECISION)
    ) * live_mask


def finish(
    potential, teacher_force, student_part, features, charge, live_mask, norm_gain, w_mix, w_read
):
    mean_square = jnp.mean(potential * potential, axis=1, keepdims=True)
    normed = (potential * lax.rsqrt(mean_square + 1e-06) * norm_gain[None, :]).astype(jnp.bfloat16)
    update = jax.nn.silu(jnp.dot(normed, w_mix, preferred_element_type=jnp.float32))
    combined = features.astype(jnp.float32) + update
    teacher_energy = jnp.dot(combined, w_read, precision=HIGHEST_PRECISION)
    student_energy = 0.5 * charge * student_part[:, 0]
    forces = charge[:, None] * student_part[:, 1:4]
    misfit = (student_energy - teacher_energy) ** 2 + jnp.sum(
        (forces - teacher_force) ** 2, axis=1
    ) / 3.0
    return (
        combined.astype(jnp.bfloat16),
        teacher_force,
        forces,
        student_energy,
        live_mask * misfit,
    )


def sum_over_atoms(payload):
    rows = lax.axis_size("y")
    width = payload.shape[1]
    parts = lax.all_to_all(payload.reshape(rows, -1, width), "y", 0, 0, tiled=True)
    along_y = jnp.sum(parts, axis=0)
    parts = lax.all_to_all(along_y, ATOM_AXES[1:], 0, 0, tiled=True)
    reduced = jnp.sum(parts, axis=0, keepdims=True)
    spread = lax.all_to_all(
        jnp.broadcast_to(reduced, along_y.shape), ATOM_AXES[1:], 0, 0, tiled=True
    )
    spread = lax.all_to_all(
        jnp.broadcast_to(spread[None], (rows,) + spread.shape), "y", 0, 0, tiled=True
    )
    return spread.reshape(payload.shape)


def sum_over_ka(payload):
    parts = lax.all_to_all(payload, "core", 1, 1, tiled=True)
    chip = jnp.sum(parts, axis=1)
    parts = lax.all_to_all(chip, "zl", 0, 0, tiled=True)
    return jnp.sum(parts, axis=0)


def sum_over_all(values):
    pair = jnp.broadcast_to(values[None, :], (lax.axis_size("core"), values.shape[0]))
    chip = jnp.sum(lax.all_to_all(pair, "core", 0, 0, tiled=True), axis=0)
    chips = 1
    for axis in ALL_AXES[:-1]:
        chips *= lax.axis_size(axis)
    copies = jnp.broadcast_to(chip[None, :], (chips, values.shape[0]))
    return jnp.sum(lax.all_to_all(copies, ALL_AXES[:-1], 0, 0, tiled=True), axis=0)


def local(
    features,
    positions,
    k_indices,
    species,
    brick_counts,
    smearing,
    teacher_charge,
    norm_gain,
    w_mix,
    w_read,
    w_student,
    species_embed,
    w_charge,
    species_bias,
    student_smear,
):
    atom_rows = features.shape[0]
    k_width = k_indices.shape[1]
    channels = features.shape[1]
    atom_groups = 1
    for axis in ATOM_AXES:
        atom_groups *= lax.axis_size(axis)
    ka_groups = 1
    for axis in KA_AXES:
        ka_groups *= lax.axis_size(axis)
    inv_root = 1.0 / math.sqrt(atom_rows * atom_groups)
    live_mask = (jnp.arange(atom_rows, dtype=jnp.int32) < brick_counts[0]).astype(jnp.float32)
    masked = features * live_mask.astype(jnp.bfloat16)[:, None]
    charge = student_charge(
        features, species, live_mask, w_student, species_embed, w_charge, species_bias
    )
    charge_low = charge.astype(jnp.bfloat16)
    phases = lax.optimization_barrier(phase_table(positions, k_indices))
    factor = lax.dot_general(
        phases, masked, (((0,), (0,)), ((), ())), preferred_element_type=jnp.float32
    )
    charge_sum = jnp.dot(charge_low, phases, preferred_element_type=jnp.float32)
    rows_each = 2 * k_width // atom_groups
    flat = rows_each * channels
    payload = jnp.concatenate(
        [factor.reshape(atom_groups, flat), charge_sum.reshape(atom_groups, rows_each)], axis=1
    )
    summed = sum_over_atoms(payload)
    factor = summed[:, :flat].reshape(2 * k_width, channels)
    charge_sum = summed[:, flat:].reshape(-1)
    k_vectors, k_square = k_geometry(k_indices)
    kernel = teacher_kernel(k_square, smearing, inv_root)
    weighted = (jnp.concatenate([kernel, kernel], axis=0) * factor).astype(jnp.bfloat16)
    potential = jnp.dot(phases, weighted, preferred_element_type=jnp.float32)
    charged = (features.astype(jnp.float32) * teacher_charge[None, :]).astype(jnp.bfloat16)
    contracted = lax.dot_general(
        charged, weighted, (((1,), (1,)), ((), ())), preferred_element_type=jnp.float32
    )
    cosines = phases[:, :k_width].astype(jnp.float32)
    sines = phases[:, k_width:].astype(jnp.float32)
    force_terms = sines * contracted[:, :k_width] - cosines * contracted[:, k_width:]
    terms_high = force_terms.astype(jnp.bfloat16)
    terms_low = (force_terms - terms_high.astype(jnp.float32)).astype(jnp.bfloat16)
    k_low = k_indices.astype(jnp.bfloat16)
    teacher_force_t = TWO_PI * (
        lax.dot_general(k_low, terms_high, (((1,), (1,)), ((), ())), preferred_element_type=jnp.float32)
        + lax.dot_general(k_low, terms_low, (((1,), (1,)), ((), ())), preferred_element_type=jnp.float32)
    )
    table = student_table(k_vectors, k_square, charge_sum, student_smear, inv_root, k_width)
    student_part_t = lax.dot_general(
        table, phases, (((0,), (1,)), ((), ())), preferred_element_type=jnp.float32
    )
    share_rows = atom_rows // ka_groups
    side = jnp.concatenate(
        [teacher_force_t, student_part_t, jnp.zeros((1, atom_rows), jnp.float32)], axis=0
    )
    side = side.reshape(8, ka_groups, share_rows).transpose(1, 0, 2)
    packed = jnp.concatenate([potential.reshape(ka_groups, share_rows, channels), side], axis=1)
    z_lo = lax.axis_size("zl")
    packed = packed.reshape(z_lo, ka_groups // z_lo, share_rows + 8, channels)
    own = sum_over_ka(packed)
    ka_index = lax.axis_index(KA_AXES)
    row_start = ka_index * share_rows

    def own_rows(values):
        return lax.dynamic_slice_in_dim(values, row_start, share_rows, 0)

    own_side = own[share_rows:].T
    teacher_features, teacher_out, forces, student_energy, misfit = finish(
        own[:share_rows],
        own_side[:, 0:3],
        own_side[:, 3:7],
        own_rows(features),
        own_rows(charge),
        own_rows(live_mask),
        norm_gain,
        w_mix,
        w_read,
    )
    totals = sum_over_all(jnp.stack([jnp.sum(misfit), jnp.sum(own_rows(live_mask))]))
    return (teacher_features, teacher_out.T, forces.T, student_energy, totals[0] / totals[1])


def solution(mesh):
    sizes = dict(mesh.shape)
    ka = sizes["ka"]
    atom = sizes["atom"]
    cores = 2
    z_lo = ka // cores
    devices = mesh.devices.reshape(-1)
    y_size = 8 if atom % 8 == 0 else 1
    rest = atom // y_size
    zh = 2 if rest % 2 == 0 else 1
    x_size = rest // zh
    fine = Mesh(devices.reshape(y_size, x_size, zh, z_lo, cores), ALL_AXES)
    atom_spec = ATOM_AXES
    in_specs = (
        P(atom_spec, None),
        P(None, atom_spec),
        P(None, KA_AXES),
        P(atom_spec),
        P(atom_spec),
        P(),
        P(),
        P(),
        P(),
        P(),
        P(),
        P(),
        P(),
        P(),
        P(),
    )
    out_specs = (
        P(ALL_AXES, None),
        P(None, ALL_AXES),
        P(None, ALL_AXES),
        P(ALL_AXES),
        P(),
    )
    return jax.shard_map(local, mesh=fine, in_specs=in_specs, out_specs=out_specs, check_vma=False)
```

```python
import math

import jax
import jax.numpy as jnp
from jax import lax
from jax.sharding import Mesh
from jax.sharding import PartitionSpec as P

TWO_PI = 2.0 * math.pi
SCREEN = 20.0
HIGHEST_PRECISION = lax.Precision.HIGHEST

ATOM_AXES = ("y", "x", "zh")
KA_AXES = ("zl", "core")
ALL_AXES = ATOM_AXES + KA_AXES


def phase_table(positions, k_indices):
    k_float = k_indices.astype(jnp.float32)
    products = (
        positions[0][:, None] * k_float[0][None, :]
        + positions[1][:, None] * k_float[1][None, :]
        + positions[2][:, None] * k_float[2][None, :]
    )
    quarters = 4.0 * products
    quarter = jnp.round(quarters)
    angle = (quarters - quarter) * (0.5 * math.pi)
    square = angle * angle
    sine = angle * (
        1.0
        + square
        * (
            -1.0 / 6.0
            + square * (1.0 / 120.0 + square * (-1.0 / 5040.0 + square * (1.0 / 362880.0)))
        )
    )
    cosine = 1.0 + square * (
        -0.5 + square * (1.0 / 24.0 + square * (-1.0 / 720.0 + square * (1.0 / 40320.0)))
    )
    turn = quarter - 4.0 * jnp.floor(quarter * 0.25)
    odd = (turn == 1.0) | (turn == 3.0)
    cos_base = jnp.where(odd, sine, cosine)
    sin_base = jnp.where(odd, cosine, sine)
    cos_value = jnp.where((turn == 1.0) | (turn == 2.0), -cos_base, cos_base)
    sin_value = jnp.where(turn >= 2.0, -sin_base, sin_base)
    return jnp.concatenate([cos_value, sin_value], axis=1).astype(jnp.bfloat16)


def k_geometry(k_indices):
    k_vectors = TWO_PI * k_indices.astype(jnp.float32)
    k_square = (
        k_vectors[0] * k_vectors[0] + k_vectors[1] * k_vectors[1] + k_vectors[2] * k_vectors[2]
    )
    return (k_vectors, k_square)


def teacher_kernel(k_square, smearing, inv_root):
    spread = (smearing * smearing)[None, :]
    return jnp.exp(-0.5 * k_square[:, None] * spread) / (k_square[:, None] + SCREEN) * inv_root


def student_table(k_vectors, k_square, sums, student_smear, inv_root, k_width):
    spread = student_smear[0] * student_smear[0]
    kernel = jnp.exp(-0.5 * k_square * spread) / (k_square + SCREEN) * inv_root
    cos_part = kernel * sums[:k_width]
    sin_part = kernel * sums[k_width:]
    upper_rows = jnp.stack(
        [
            cos_part,
            -(k_vectors[0] * sin_part),
            -(k_vectors[1] * sin_part),
            -(k_vectors[2] * sin_part),
        ],
        axis=1,
    )
    lower_rows = jnp.stack(
        [sin_part, k_vectors[0] * cos_part, k_vectors[1] * cos_part, k_vectors[2] * cos_part],
        axis=1,
    )
    return jnp.concatenate([upper_rows, lower_rows], axis=0).astype(jnp.bfloat16)


def student_charge(features, species, live_mask, w_student, species_embed, w_charge, species_bias):
    onehot = (
        species[:, None] == jnp.arange(species_embed.shape[0], dtype=jnp.int32)[None, :]
    ).astype(jnp.float32)
    inner_sum = jnp.dot(features, w_student, preferred_element_type=jnp.float32) + jnp.dot(
        onehot, species_embed, precision=HIGHEST_PRECISION
    )
    hidden = jax.nn.silu(inner_sum)
    return (
        jnp.dot(hidden, w_charge, precision=HIGHEST_PRECISION)
        + jnp.dot(onehot, species_bias, precision=HIGHEST_PRECISION)
    ) * live_mask


def finish(
    potential, teacher_force, student_part, features, charge, live_mask, norm_gain, w_mix, w_read
):
    mean_square = jnp.mean(potential * potential, axis=1, keepdims=True)
    normed = (potential * lax.rsqrt(mean_square + 1e-06) * norm_gain[None, :]).astype(jnp.bfloat16)
    update = jax.nn.silu(jnp.dot(normed, w_mix, preferred_element_type=jnp.float32))
    combined = features.astype(jnp.float32) + update
    teacher_energy = jnp.dot(combined, w_read, precision=HIGHEST_PRECISION)
    student_energy = 0.5 * charge * student_part[:, 0]
    forces = charge[:, None] * student_part[:, 1:4]
    misfit = (student_energy - teacher_energy) ** 2 + jnp.sum(
        (forces - teacher_force) ** 2, axis=1
    ) / 3.0
    return (
        combined.astype(jnp.bfloat16),
        teacher_force,
        forces,
        student_energy,
        live_mask * misfit,
    )


def sum_over_atoms(payload, finish_chunk):
    parts = lax.all_to_all(payload, ATOM_AXES, 0, 0, tiled=True)
    reduced = finish_chunk(jnp.sum(parts, axis=0))
    spread = jnp.broadcast_to(reduced[None, :], payload.shape)
    return lax.all_to_all(spread, ATOM_AXES, 0, 0, tiled=True)


def sum_over_ka(payload):
    parts = lax.all_to_all(payload, "core", 1, 1, tiled=True)
    chip = jnp.sum(parts, axis=1)
    parts = lax.all_to_all(chip, "zl", 0, 0, tiled=True)
    return jnp.sum(parts, axis=0)


def sum_over_all(values):
    pair = jnp.broadcast_to(values[None, :], (lax.axis_size("core"), values.shape[0]))
    chip = jnp.sum(lax.all_to_all(pair, "core", 0, 0, tiled=True), axis=0)
    chips = 1
    for axis in ALL_AXES[:-1]:
        chips *= lax.axis_size(axis)
    copies = jnp.broadcast_to(chip[None, :], (chips, values.shape[0]))
    return jnp.sum(lax.all_to_all(copies, ALL_AXES[:-1], 0, 0, tiled=True), axis=0)


def local(
    features,
    positions,
    k_indices,
    species,
    brick_counts,
    smearing,
    teacher_charge,
    norm_gain,
    w_mix,
    w_read,
    w_student,
    species_embed,
    w_charge,
    species_bias,
    student_smear,
):
    atom_rows = features.shape[0]
    k_width = k_indices.shape[1]
    channels = features.shape[1]
    atom_groups = 1
    for axis in ATOM_AXES:
        atom_groups *= lax.axis_size(axis)
    ka_groups = 1
    for axis in KA_AXES:
        ka_groups *= lax.axis_size(axis)
    inv_root = 1.0 / math.sqrt(atom_rows * atom_groups)
    live_mask = (jnp.arange(atom_rows, dtype=jnp.int32) < brick_counts[0]).astype(jnp.float32)
    masked = features * live_mask.astype(jnp.bfloat16)[:, None]
    charge = student_charge(
        features, species, live_mask, w_student, species_embed, w_charge, species_bias
    )
    charge_low = charge.astype(jnp.bfloat16)
    phases = lax.optimization_barrier(phase_table(positions, k_indices))
    factor = lax.dot_general(
        phases, masked, (((0,), (0,)), ((), ())), preferred_element_type=jnp.float32
    )
    charge_sum = jnp.dot(charge_low, phases, preferred_element_type=jnp.float32)
    rows_each = 2 * k_width // atom_groups
    flat = rows_each * channels
    payload = jnp.concatenate(
        [factor.reshape(atom_groups, flat), charge_sum.reshape(atom_groups, rows_each)], axis=1
    )
    k_vectors, k_square = k_geometry(k_indices)
    owner = lax.axis_index(ATOM_AXES)
    k_start = (owner * rows_each) % k_width

    def weigh(chunk):
        chunk_square = lax.dynamic_slice_in_dim(k_square, k_start, rows_each, 0)
        chunk_kernel = teacher_kernel(chunk_square, smearing, inv_root)
        rows = chunk[:flat].reshape(rows_each, channels)
        rounded = (chunk_kernel * rows).astype(jnp.bfloat16).astype(jnp.float32)
        return jnp.concatenate([rounded.reshape(-1), chunk[flat:]])

    summed = sum_over_atoms(payload, weigh)
    weighted = summed[:, :flat].reshape(2 * k_width, channels).astype(jnp.bfloat16)
    charge_sum = summed[:, flat:].reshape(-1)
    potential = jnp.dot(phases, weighted, preferred_element_type=jnp.float32)
    charged = (features.astype(jnp.float32) * teacher_charge[None, :]).astype(jnp.bfloat16)
    contracted = lax.dot_general(
        charged, weighted, (((1,), (1,)), ((), ())), preferred_element_type=jnp.float32
    )
    cosines = phases[:, :k_width].astype(jnp.float32)
    sines = phases[:, k_width:].astype(jnp.float32)
    force_terms = sines * contracted[:, :k_width] - cosines * contracted[:, k_width:]
    terms_high = force_terms.astype(jnp.bfloat16)
    terms_low = (force_terms - terms_high.astype(jnp.float32)).astype(jnp.bfloat16)
    k_low = k_indices.astype(jnp.bfloat16)
    teacher_force_t = TWO_PI * (
        lax.dot_general(k_low, terms_high, (((1,), (1,)), ((), ())), preferred_element_type=jnp.float32)
        + lax.dot_general(k_low, terms_low, (((1,), (1,)), ((), ())), preferred_element_type=jnp.float32)
    )
    table = student_table(k_vectors, k_square, charge_sum, student_smear, inv_root, k_width)
    student_part_t = lax.dot_general(
        table, phases, (((0,), (1,)), ((), ())), preferred_element_type=jnp.float32
    )
    share_rows = atom_rows // ka_groups
    side = jnp.concatenate(
        [teacher_force_t, student_part_t, jnp.zeros((1, atom_rows), jnp.float32)], axis=0
    )
    side = side.reshape(8, ka_groups, share_rows).transpose(1, 0, 2)
    packed = jnp.concatenate([potential.reshape(ka_groups, share_rows, channels), side], axis=1)
    z_lo = lax.axis_size("zl")
    packed = packed.reshape(z_lo, ka_groups // z_lo, share_rows + 8, channels)
    own = sum_over_ka(packed)
    ka_index = lax.axis_index(KA_AXES)
    row_start = ka_index * share_rows

    def own_rows(values):
        return lax.dynamic_slice_in_dim(values, row_start, share_rows, 0)

    own_side = own[share_rows:].T
    teacher_features, teacher_out, forces, student_energy, misfit = finish(
        own[:share_rows],
        own_side[:, 0:3],
        own_side[:, 3:7],
        own_rows(features),
        own_rows(charge),
        own_rows(live_mask),
        norm_gain,
        w_mix,
        w_read,
    )
    totals = sum_over_all(jnp.stack([jnp.sum(misfit), jnp.sum(own_rows(live_mask))]))
    return (teacher_features, teacher_out.T, forces.T, student_energy, totals[0] / totals[1])


def solution(mesh):
    sizes = dict(mesh.shape)
    ka = sizes["ka"]
    atom = sizes["atom"]
    cores = 2
    z_lo = ka // cores
    devices = mesh.devices.reshape(-1)
    y_size = 8 if atom % 8 == 0 else 1
    rest = atom // y_size
    zh = 2 if rest % 2 == 0 else 1
    x_size = rest // zh
    fine = Mesh(devices.reshape(y_size, x_size, zh, z_lo, cores), ALL_AXES)
    atom_spec = ATOM_AXES
    in_specs = (
        P(atom_spec, None),
        P(None, atom_spec),
        P(None, KA_AXES),
        P(atom_spec),
        P(atom_spec),
        P(),
        P(),
        P(),
        P(),
        P(),
        P(),
        P(),
        P(),
        P(),
        P(),
    )
    out_specs = (
        P(ALL_AXES, None),
        P(None, ALL_AXES),
        P(None, ALL_AXES),
        P(ALL_AXES),
        P(),
    )
    return jax.shard_map(local, mesh=fine, in_specs=in_specs, out_specs=out_specs, check_vma=False)
```

```python
import math

import jax
import jax.numpy as jnp
from jax import lax
from jax.sharding import Mesh
from jax.sharding import PartitionSpec as P

TWO_PI = 2.0 * math.pi
SCREEN = 20.0
HIGHEST_PRECISION = lax.Precision.HIGHEST

ATOM_AXES = ("y", "x", "zh")
KA_AXES = ("zl", "core")
ALL_AXES = ATOM_AXES + KA_AXES


def phase_table(positions, k_indices):
    k_float = k_indices.astype(jnp.float32)
    products = (
        positions[0][:, None] * k_float[0][None, :]
        + positions[1][:, None] * k_float[1][None, :]
        + positions[2][:, None] * k_float[2][None, :]
    )
    quarters = 4.0 * products
    quarter = jnp.round(quarters)
    angle = (quarters - quarter) * (0.5 * math.pi)
    square = angle * angle
    sine = angle * (
        1.0
        + square
        * (
            -1.0 / 6.0
            + square * (1.0 / 120.0 + square * (-1.0 / 5040.0 + square * (1.0 / 362880.0)))
        )
    )
    cosine = 1.0 + square * (
        -0.5 + square * (1.0 / 24.0 + square * (-1.0 / 720.0 + square * (1.0 / 40320.0)))
    )
    turn = quarter - 4.0 * jnp.floor(quarter * 0.25)
    odd = (turn == 1.0) | (turn == 3.0)
    cos_base = jnp.where(odd, sine, cosine)
    sin_base = jnp.where(odd, cosine, sine)
    cos_value = jnp.where((turn == 1.0) | (turn == 2.0), -cos_base, cos_base)
    sin_value = jnp.where(turn >= 2.0, -sin_base, sin_base)
    return jnp.concatenate([cos_value, sin_value], axis=1).astype(jnp.bfloat16)


def k_geometry(k_indices):
    k_vectors = TWO_PI * k_indices.astype(jnp.float32)
    k_square = (
        k_vectors[0] * k_vectors[0] + k_vectors[1] * k_vectors[1] + k_vectors[2] * k_vectors[2]
    )
    return (k_vectors, k_square)


def teacher_kernel(k_square, smearing, inv_root):
    spread = (smearing * smearing)[None, :]
    return jnp.exp(-0.5 * k_square[:, None] * spread) / (k_square[:, None] + SCREEN) * inv_root


def student_table(k_vectors, k_square, sums, student_smear, inv_root, k_width):
    spread = student_smear[0] * student_smear[0]
    kernel = jnp.exp(-0.5 * k_square * spread) / (k_square + SCREEN) * inv_root
    cos_part = kernel * sums[:k_width]
    sin_part = kernel * sums[k_width:]
    upper_rows = jnp.stack(
        [
            cos_part,
            -(k_vectors[0] * sin_part),
            -(k_vectors[1] * sin_part),
            -(k_vectors[2] * sin_part),
        ],
        axis=1,
    )
    lower_rows = jnp.stack(
        [sin_part, k_vectors[0] * cos_part, k_vectors[1] * cos_part, k_vectors[2] * cos_part],
        axis=1,
    )
    return jnp.concatenate([upper_rows, lower_rows], axis=0).astype(jnp.bfloat16)


def student_charge(features, species, live_mask, w_student, species_embed, w_charge, species_bias):
    onehot = (
        species[:, None] == jnp.arange(species_embed.shape[0], dtype=jnp.int32)[None, :]
    ).astype(jnp.float32)
    inner_sum = jnp.dot(features, w_student, preferred_element_type=jnp.float32) + jnp.dot(
        onehot, species_embed, precision=HIGHEST_PRECISION
    )
    hidden = jax.nn.silu(inner_sum)
    return (
        jnp.dot(hidden, w_charge, precision=HIGHEST_PRECISION)
        + jnp.dot(onehot, species_bias, precision=HIGHEST_PRECISION)
    ) * live_mask


def finish(
    potential, teacher_force, student_part, features, charge, live_mask, norm_gain, w_mix, w_read
):
    mean_square = jnp.mean(potential * potential, axis=1, keepdims=True)
    normed = (potential * lax.rsqrt(mean_square + 1e-06) * norm_gain[None, :]).astype(jnp.bfloat16)
    update = jax.nn.silu(jnp.dot(normed, w_mix, preferred_element_type=jnp.float32))
    combined = features.astype(jnp.float32) + update
    teacher_energy = jnp.dot(combined, w_read, precision=HIGHEST_PRECISION)
    student_energy = 0.5 * charge * student_part[:, 0]
    forces = charge[:, None] * student_part[:, 1:4]
    misfit = (student_energy - teacher_energy) ** 2 + jnp.sum(
        (forces - teacher_force) ** 2, axis=1
    ) / 3.0
    return (
        combined.astype(jnp.bfloat16),
        teacher_force,
        forces,
        student_energy,
        live_mask * misfit,
    )


def sum_over_atoms(payload, finish_chunk):
    parts = lax.all_to_all(payload, ATOM_AXES, 0, 0, tiled=True)
    reduced = finish_chunk(jnp.sum(parts, axis=0))
    spread = jnp.broadcast_to(reduced[None, :], payload.shape)
    return lax.all_to_all(spread, ATOM_AXES, 0, 0, tiled=True)


def sum_over_ka(payload):
    parts = lax.all_to_all(payload, "core", 1, 1, tiled=True)
    chip = jnp.sum(parts, axis=1)
    parts = lax.all_to_all(chip, "zl", 0, 0, tiled=True)
    return jnp.sum(parts, axis=0)


def sum_over_all(values):
    pair = jnp.broadcast_to(values[None, :], (lax.axis_size("core"), values.shape[0]))
    chip = jnp.sum(lax.all_to_all(pair, "core", 0, 0, tiled=True), axis=0)
    chips = 1
    for axis in ALL_AXES[:-1]:
        chips *= lax.axis_size(axis)
    copies = jnp.broadcast_to(chip[None, :], (chips, values.shape[0]))
    return jnp.sum(lax.all_to_all(copies, ALL_AXES[:-1], 0, 0, tiled=True), axis=0)


def local(
    features,
    positions,
    k_indices,
    species,
    brick_counts,
    smearing,
    teacher_charge,
    norm_gain,
    w_mix,
    w_read,
    w_student,
    species_embed,
    w_charge,
    species_bias,
    student_smear,
):
    atom_rows = features.shape[0]
    k_width = k_indices.shape[1]
    channels = features.shape[1]
    atom_groups = 1
    for axis in ATOM_AXES:
        atom_groups *= lax.axis_size(axis)
    ka_groups = 1
    for axis in KA_AXES:
        ka_groups *= lax.axis_size(axis)
    inv_root = 1.0 / math.sqrt(atom_rows * atom_groups)
    live_mask = (jnp.arange(atom_rows, dtype=jnp.int32) < brick_counts[0]).astype(jnp.float32)
    masked = features * live_mask.astype(jnp.bfloat16)[:, None]
    charge = student_charge(
        features, species, live_mask, w_student, species_embed, w_charge, species_bias
    )
    charge_low = charge.astype(jnp.bfloat16)
    phases = lax.optimization_barrier(phase_table(positions, k_indices))
    factor = lax.dot_general(
        phases, masked, (((0,), (0,)), ((), ())), preferred_element_type=jnp.float32
    )
    charge_sum = jnp.dot(charge_low, phases, preferred_element_type=jnp.float32)
    rows_each = 2 * k_width // atom_groups
    flat = rows_each * channels
    payload = jnp.concatenate(
        [factor.reshape(atom_groups, flat), charge_sum.reshape(atom_groups, rows_each)], axis=1
    )
    k_vectors, k_square = k_geometry(k_indices)
    owner = lax.axis_index(ATOM_AXES)
    k_start = (owner * rows_each) % k_width

    def weigh(chunk):
        chunk_square = lax.dynamic_slice_in_dim(k_square, k_start, rows_each, 0)
        chunk_kernel = teacher_kernel(chunk_square, smearing, inv_root)
        rows = chunk[:flat].reshape(rows_each, channels)
        rounded = (chunk_kernel * rows).astype(jnp.bfloat16).astype(jnp.float32)
        return jnp.concatenate([rounded.reshape(-1), chunk[flat:]])

    summed = sum_over_atoms(payload, weigh)
    weighted = summed[:, :flat].reshape(2 * k_width, channels).astype(jnp.bfloat16)
    charge_sum = summed[:, flat:].reshape(-1)
    potential = jnp.dot(phases, weighted, preferred_element_type=jnp.float32)
    charged = (features.astype(jnp.float32) * teacher_charge[None, :]).astype(jnp.bfloat16)
    contracted = lax.dot_general(
        charged, weighted, (((1,), (1,)), ((), ())), preferred_element_type=jnp.float32
    )
    cosines = phases[:, :k_width].astype(jnp.float32)
    sines = phases[:, k_width:].astype(jnp.float32)
    force_terms = sines * contracted[:, :k_width] - cosines * contracted[:, k_width:]
    terms_high = force_terms.astype(jnp.bfloat16)
    terms_low = (force_terms - terms_high.astype(jnp.float32)).astype(jnp.bfloat16)
    k_low = k_indices.astype(jnp.bfloat16)
    terms = jnp.concatenate([terms_high, terms_low], axis=1)
    teacher_force_t = TWO_PI * lax.dot_general(
        jnp.concatenate([k_low, k_low], axis=1),
        terms,
        (((1,), (1,)), ((), ())),
        preferred_element_type=jnp.float32,
    )
    table = student_table(k_vectors, k_square, charge_sum, student_smear, inv_root, k_width)
    student_part_t = lax.dot_general(
        table, phases, (((0,), (1,)), ((), ())), preferred_element_type=jnp.float32
    )
    share_rows = atom_rows // ka_groups
    side = jnp.concatenate(
        [teacher_force_t, student_part_t, jnp.zeros((1, atom_rows), jnp.float32)], axis=0
    )
    side = side.reshape(8, ka_groups, share_rows).transpose(1, 0, 2)
    packed = jnp.concatenate([potential.reshape(ka_groups, share_rows, channels), side], axis=1)
    z_lo = lax.axis_size("zl")
    packed = packed.reshape(z_lo, ka_groups // z_lo, share_rows + 8, channels)
    own = sum_over_ka(packed)
    ka_index = lax.axis_index(KA_AXES)
    row_start = ka_index * share_rows

    def own_rows(values):
        return lax.dynamic_slice_in_dim(values, row_start, share_rows, 0)

    own_side = own[share_rows:].T
    teacher_features, teacher_out, forces, student_energy, misfit = finish(
        own[:share_rows],
        own_side[:, 0:3],
        own_side[:, 3:7],
        own_rows(features),
        own_rows(charge),
        own_rows(live_mask),
        norm_gain,
        w_mix,
        w_read,
    )
    totals = sum_over_all(jnp.stack([jnp.sum(misfit), jnp.sum(own_rows(live_mask))]))
    return (teacher_features, teacher_out.T, forces.T, student_energy, totals[0] / totals[1])


def solution(mesh):
    sizes = dict(mesh.shape)
    ka = sizes["ka"]
    atom = sizes["atom"]
    cores = 2
    z_lo = ka // cores
    devices = mesh.devices.reshape(-1)
    y_size = 8 if atom % 8 == 0 else 1
    rest = atom // y_size
    zh = 2 if rest % 2 == 0 else 1
    x_size = rest // zh
    fine = Mesh(devices.reshape(y_size, x_size, zh, z_lo, cores), ALL_AXES)
    atom_spec = ATOM_AXES
    in_specs = (
        P(atom_spec, None),
        P(None, atom_spec),
        P(None, KA_AXES),
        P(atom_spec),
        P(atom_spec),
        P(),
        P(),
        P(),
        P(),
        P(),
        P(),
        P(),
        P(),
        P(),
        P(),
    )
    out_specs = (
        P(ALL_AXES, None),
        P(None, ALL_AXES),
        P(None, ALL_AXES),
        P(ALL_AXES),
        P(),
    )
    return jax.shard_map(local, mesh=fine, in_specs=in_specs, out_specs=out_specs, check_vma=False)
```

```python
import math

import jax
import jax.numpy as jnp
from jax import lax
from jax.sharding import Mesh
from jax.sharding import PartitionSpec as P

TWO_PI = 2.0 * math.pi
SCREEN = 20.0
HIGHEST_PRECISION = lax.Precision.HIGHEST

ATOM_AXES = ("y", "x", "zh")
KA_AXES = ("zl", "core")
ALL_AXES = ATOM_AXES + KA_AXES


def phase_table(positions, k_indices):
    k_float = k_indices.astype(jnp.float32)
    products = (
        positions[0][:, None] * k_float[0][None, :]
        + positions[1][:, None] * k_float[1][None, :]
        + positions[2][:, None] * k_float[2][None, :]
    )
    quarters = 4.0 * products
    quarter = jnp.round(quarters)
    angle = (quarters - quarter) * (0.5 * math.pi)
    square = angle * angle
    sine = angle * (
        1.0
        + square
        * (
            -1.0 / 6.0
            + square * (1.0 / 120.0 + square * (-1.0 / 5040.0 + square * (1.0 / 362880.0)))
        )
    )
    cosine = 1.0 + square * (
        -0.5 + square * (1.0 / 24.0 + square * (-1.0 / 720.0 + square * (1.0 / 40320.0)))
    )
    turn = quarter - 4.0 * jnp.floor(quarter * 0.25)
    odd = (turn == 1.0) | (turn == 3.0)
    cos_base = jnp.where(odd, sine, cosine)
    sin_base = jnp.where(odd, cosine, sine)
    cos_value = jnp.where((turn == 1.0) | (turn == 2.0), -cos_base, cos_base)
    sin_value = jnp.where(turn >= 2.0, -sin_base, sin_base)
    return jnp.concatenate([cos_value, sin_value], axis=1).astype(jnp.bfloat16)


def k_geometry(k_indices):
    k_vectors = TWO_PI * k_indices.astype(jnp.float32)
    k_square = (
        k_vectors[0] * k_vectors[0] + k_vectors[1] * k_vectors[1] + k_vectors[2] * k_vectors[2]
    )
    return (k_vectors, k_square)


def teacher_kernel(k_square, smearing, inv_root):
    spread = (smearing * smearing)[None, :]
    return jnp.exp(-0.5 * k_square[:, None] * spread) / (k_square[:, None] + SCREEN) * inv_root


def student_table(k_vectors, k_square, sums, student_smear, inv_root, k_width):
    spread = student_smear[0] * student_smear[0]
    kernel = jnp.exp(-0.5 * k_square * spread) / (k_square + SCREEN) * inv_root
    cos_part = kernel * sums[:k_width]
    sin_part = kernel * sums[k_width:]
    upper_rows = jnp.stack(
        [
            cos_part,
            -(k_vectors[0] * sin_part),
            -(k_vectors[1] * sin_part),
            -(k_vectors[2] * sin_part),
        ],
        axis=1,
    )
    lower_rows = jnp.stack(
        [sin_part, k_vectors[0] * cos_part, k_vectors[1] * cos_part, k_vectors[2] * cos_part],
        axis=1,
    )
    return jnp.concatenate([upper_rows, lower_rows], axis=0).astype(jnp.bfloat16)


def student_charge(features, species, live_mask, w_student, species_embed, w_charge, species_bias):
    embed = jnp.zeros((features.shape[0], species_embed.shape[1]), jnp.float32)
    bias = jnp.zeros((features.shape[0],), jnp.float32)
    for kind in range(species_embed.shape[0]):
        chosen = species == kind
        embed = embed + jnp.where(chosen[:, None], species_embed[kind][None, :], 0.0)
        bias = bias + jnp.where(chosen, species_bias[kind], 0.0)
    inner_sum = jnp.dot(features, w_student, preferred_element_type=jnp.float32) + embed
    hidden = jax.nn.silu(inner_sum)
    return (jnp.dot(hidden, w_charge, precision=HIGHEST_PRECISION) + bias) * live_mask


def finish(
    potential, teacher_force, student_part, features, charge, live_mask, norm_gain, w_mix, w_read
):
    mean_square = jnp.mean(potential * potential, axis=1, keepdims=True)
    normed = (potential * lax.rsqrt(mean_square + 1e-06) * norm_gain[None, :]).astype(jnp.bfloat16)
    update = jax.nn.silu(jnp.dot(normed, w_mix, preferred_element_type=jnp.float32))
    combined = features.astype(jnp.float32) + update
    teacher_energy = jnp.dot(combined, w_read, precision=HIGHEST_PRECISION)
    student_energy = 0.5 * charge * student_part[:, 0]
    forces = charge[:, None] * student_part[:, 1:4]
    misfit = (student_energy - teacher_energy) ** 2 + jnp.sum(
        (forces - teacher_force) ** 2, axis=1
    ) / 3.0
    return (
        combined.astype(jnp.bfloat16),
        teacher_force,
        forces,
        student_energy,
        live_mask * misfit,
    )


def sum_over_atoms(payload, finish_chunk):
    parts = lax.all_to_all(payload, ATOM_AXES, 0, 0, tiled=True)
    reduced = finish_chunk(jnp.sum(parts, axis=0))
    spread = jnp.broadcast_to(reduced[None, :], payload.shape)
    return lax.all_to_all(spread, ATOM_AXES, 0, 0, tiled=True)


def sum_over_ka(payload):
    parts = lax.all_to_all(payload, "core", 1, 1, tiled=True)
    chip = jnp.sum(parts, axis=1)
    parts = lax.all_to_all(chip, "zl", 0, 0, tiled=True)
    return jnp.sum(parts, axis=0)


def sum_over_all(values):
    pair = jnp.broadcast_to(values[None, :], (lax.axis_size("core"), values.shape[0]))
    chip = jnp.sum(lax.all_to_all(pair, "core", 0, 0, tiled=True), axis=0)
    chips = 1
    for axis in ALL_AXES[:-1]:
        chips *= lax.axis_size(axis)
    copies = jnp.broadcast_to(chip[None, :], (chips, values.shape[0]))
    return jnp.sum(lax.all_to_all(copies, ALL_AXES[:-1], 0, 0, tiled=True), axis=0)


def local(
    features,
    positions,
    k_indices,
    species,
    brick_counts,
    smearing,
    teacher_charge,
    norm_gain,
    w_mix,
    w_read,
    w_student,
    species_embed,
    w_charge,
    species_bias,
    student_smear,
):
    atom_rows = features.shape[0]
    k_width = k_indices.shape[1]
    channels = features.shape[1]
    atom_groups = 1
    for axis in ATOM_AXES:
        atom_groups *= lax.axis_size(axis)
    ka_groups = 1
    for axis in KA_AXES:
        ka_groups *= lax.axis_size(axis)
    inv_root = 1.0 / math.sqrt(atom_rows * atom_groups)
    live_mask = (jnp.arange(atom_rows, dtype=jnp.int32) < brick_counts[0]).astype(jnp.float32)
    masked = features * live_mask.astype(jnp.bfloat16)[:, None]
    charge = student_charge(
        features, species, live_mask, w_student, species_embed, w_charge, species_bias
    )
    charge_low = charge.astype(jnp.bfloat16)
    phases = lax.optimization_barrier(phase_table(positions, k_indices))
    factor = lax.dot_general(
        phases, masked, (((0,), (0,)), ((), ())), preferred_element_type=jnp.float32
    )
    charge_sum = jnp.dot(charge_low, phases, preferred_element_type=jnp.float32)
    rows_each = 2 * k_width // atom_groups
    flat = rows_each * channels
    payload = jnp.concatenate(
        [factor.reshape(atom_groups, flat), charge_sum.reshape(atom_groups, rows_each)], axis=1
    )
    k_vectors, k_square = k_geometry(k_indices)
    owner = lax.axis_index(ATOM_AXES)
    k_start = (owner * rows_each) % k_width

    def weigh(chunk):
        chunk_square = lax.dynamic_slice_in_dim(k_square, k_start, rows_each, 0)
        chunk_kernel = teacher_kernel(chunk_square, smearing, inv_root)
        rows = chunk[:flat].reshape(rows_each, channels)
        rounded = (chunk_kernel * rows).astype(jnp.bfloat16).astype(jnp.float32)
        return jnp.concatenate([rounded.reshape(-1), chunk[flat:]])

    summed = sum_over_atoms(payload, weigh)
    weighted = summed[:, :flat].reshape(2 * k_width, channels).astype(jnp.bfloat16)
    charge_sum = summed[:, flat:].reshape(-1)
    potential = jnp.dot(phases, weighted, preferred_element_type=jnp.float32)
    charged = (features.astype(jnp.float32) * teacher_charge[None, :]).astype(jnp.bfloat16)
    contracted = lax.dot_general(
        charged, weighted, (((1,), (1,)), ((), ())), preferred_element_type=jnp.float32
    )
    cosines = phases[:, :k_width].astype(jnp.float32)
    sines = phases[:, k_width:].astype(jnp.float32)
    force_terms = sines * contracted[:, :k_width] - cosines * contracted[:, k_width:]
    terms_high = force_terms.astype(jnp.bfloat16)
    terms_low = (force_terms - terms_high.astype(jnp.float32)).astype(jnp.bfloat16)
    k_low = k_indices.astype(jnp.bfloat16)
    terms = jnp.concatenate([terms_high, terms_low], axis=1)
    teacher_force_t = TWO_PI * lax.dot_general(
        jnp.concatenate([k_low, k_low], axis=1),
        terms,
        (((1,), (1,)), ((), ())),
        preferred_element_type=jnp.float32,
    )
    table = student_table(k_vectors, k_square, charge_sum, student_smear, inv_root, k_width)
    student_part_t = lax.dot_general(
        table, phases, (((0,), (1,)), ((), ())), preferred_element_type=jnp.float32
    )
    share_rows = atom_rows // ka_groups
    side = jnp.concatenate(
        [teacher_force_t, student_part_t, jnp.zeros((1, atom_rows), jnp.float32)], axis=0
    )
    side = side.reshape(8, ka_groups, share_rows).transpose(1, 0, 2)
    packed = jnp.concatenate([potential.reshape(ka_groups, share_rows, channels), side], axis=1)
    z_lo = lax.axis_size("zl")
    packed = packed.reshape(z_lo, ka_groups // z_lo, share_rows + 8, channels)
    own = sum_over_ka(packed)
    ka_index = lax.axis_index(KA_AXES)
    row_start = ka_index * share_rows

    def own_rows(values):
        return lax.dynamic_slice_in_dim(values, row_start, share_rows, 0)

    own_side = own[share_rows:].T
    teacher_features, teacher_out, forces, student_energy, misfit = finish(
        own[:share_rows],
        own_side[:, 0:3],
        own_side[:, 3:7],
        own_rows(features),
        own_rows(charge),
        own_rows(live_mask),
        norm_gain,
        w_mix,
        w_read,
    )
    totals = sum_over_all(jnp.stack([jnp.sum(misfit), jnp.sum(own_rows(live_mask))]))
    return (teacher_features, teacher_out.T, forces.T, student_energy, totals[0] / totals[1])


def solution(mesh):
    sizes = dict(mesh.shape)
    ka = sizes["ka"]
    atom = sizes["atom"]
    cores = 2
    z_lo = ka // cores
    devices = mesh.devices.reshape(-1)
    y_size = 8 if atom % 8 == 0 else 1
    rest = atom // y_size
    zh = 2 if rest % 2 == 0 else 1
    x_size = rest // zh
    fine = Mesh(devices.reshape(y_size, x_size, zh, z_lo, cores), ALL_AXES)
    atom_spec = ATOM_AXES
    in_specs = (
        P(atom_spec, None),
        P(None, atom_spec),
        P(None, KA_AXES),
        P(atom_spec),
        P(atom_spec),
        P(),
        P(),
        P(),
        P(),
        P(),
        P(),
        P(),
        P(),
        P(),
        P(),
    )
    out_specs = (
        P(ALL_AXES, None),
        P(None, ALL_AXES),
        P(None, ALL_AXES),
        P(ALL_AXES),
        P(),
    )
    return jax.shard_map(local, mesh=fine, in_specs=in_specs, out_specs=out_specs, check_vma=False)
```

```python
import math

import jax
import jax.numpy as jnp
from jax import lax
from jax.sharding import Mesh
from jax.sharding import PartitionSpec as P

TWO_PI = 2.0 * math.pi
SCREEN = 20.0
HIGHEST_PRECISION = lax.Precision.HIGHEST

ATOM_AXES = ("y", "x", "zh")
KA_AXES = ("zl", "core")
ALL_AXES = ATOM_AXES + KA_AXES


def phase_table(positions, k_indices):
    k_float = k_indices.astype(jnp.float32)
    products = (
        positions[0][:, None] * k_float[0][None, :]
        + positions[1][:, None] * k_float[1][None, :]
        + positions[2][:, None] * k_float[2][None, :]
    )
    quarters = 4.0 * products
    quarter = jnp.round(quarters)
    angle = (quarters - quarter) * (0.5 * math.pi)
    square = angle * angle
    sine = angle * (
        1.0
        + square
        * (
            -1.0 / 6.0
            + square * (1.0 / 120.0 + square * (-1.0 / 5040.0 + square * (1.0 / 362880.0)))
        )
    )
    cosine = 1.0 + square * (
        -0.5 + square * (1.0 / 24.0 + square * (-1.0 / 720.0 + square * (1.0 / 40320.0)))
    )
    turn = quarter - 4.0 * jnp.floor(quarter * 0.25)
    odd = (turn == 1.0) | (turn == 3.0)
    cos_base = jnp.where(odd, sine, cosine)
    sin_base = jnp.where(odd, cosine, sine)
    cos_value = jnp.where((turn == 1.0) | (turn == 2.0), -cos_base, cos_base)
    sin_value = jnp.where(turn >= 2.0, -sin_base, sin_base)
    return jnp.concatenate([cos_value, sin_value], axis=1).astype(jnp.bfloat16)


def k_geometry(k_indices):
    k_vectors = TWO_PI * k_indices.astype(jnp.float32)
    k_square = (
        k_vectors[0] * k_vectors[0] + k_vectors[1] * k_vectors[1] + k_vectors[2] * k_vectors[2]
    )
    return (k_vectors, k_square)


def teacher_kernel(k_square, smearing, inv_root):
    spread = (smearing * smearing)[None, :]
    return jnp.exp(-0.5 * k_square[:, None] * spread) / (k_square[:, None] + SCREEN) * inv_root


def student_table(k_vectors, k_square, sums, student_smear, inv_root, k_width):
    spread = student_smear[0] * student_smear[0]
    kernel = jnp.exp(-0.5 * k_square * spread) / (k_square + SCREEN) * inv_root
    cos_part = kernel * sums[:k_width]
    sin_part = kernel * sums[k_width:]
    upper_rows = jnp.stack(
        [
            cos_part,
            -(k_vectors[0] * sin_part),
            -(k_vectors[1] * sin_part),
            -(k_vectors[2] * sin_part),
        ],
        axis=1,
    )
    lower_rows = jnp.stack(
        [sin_part, k_vectors[0] * cos_part, k_vectors[1] * cos_part, k_vectors[2] * cos_part],
        axis=1,
    )
    return jnp.concatenate([upper_rows, lower_rows], axis=0).astype(jnp.bfloat16)


def student_charge(features, species, live_mask, w_student, species_embed, w_charge, species_bias):
    onehot = (
        species[:, None] == jnp.arange(species_embed.shape[0], dtype=jnp.int32)[None, :]
    ).astype(jnp.float32)
    inner_sum = jnp.dot(features, w_student, preferred_element_type=jnp.float32) + jnp.dot(
        onehot, species_embed, precision=HIGHEST_PRECISION
    )
    hidden = jax.nn.silu(inner_sum)
    return (
        jnp.sum(hidden * w_charge[None, :], axis=1)
        + jnp.dot(onehot, species_bias, precision=HIGHEST_PRECISION)
    ) * live_mask


def finish(
    potential, teacher_force, student_part, features, charge, live_mask, norm_gain, w_mix, w_read
):
    mean_square = jnp.mean(potential * potential, axis=1, keepdims=True)
    normed = (potential * lax.rsqrt(mean_square + 1e-06) * norm_gain[None, :]).astype(jnp.bfloat16)
    update = jax.nn.silu(jnp.dot(normed, w_mix, preferred_element_type=jnp.float32))
    combined = features.astype(jnp.float32) + update
    teacher_energy = jnp.dot(combined, w_read, precision=HIGHEST_PRECISION)
    student_energy = 0.5 * charge * student_part[:, 0]
    forces = charge[:, None] * student_part[:, 1:4]
    misfit = (student_energy - teacher_energy) ** 2 + jnp.sum(
        (forces - teacher_force) ** 2, axis=1
    ) / 3.0
    return (
        combined.astype(jnp.bfloat16),
        teacher_force,
        forces,
        student_energy,
        live_mask * misfit,
    )


def sum_over_atoms(payload, finish_chunk):
    parts = lax.all_to_all(payload, ATOM_AXES, 0, 0, tiled=True)
    reduced = finish_chunk(jnp.sum(parts, axis=0))
    spread = jnp.broadcast_to(reduced[None, :], payload.shape)
    return lax.all_to_all(spread, ATOM_AXES, 0, 0, tiled=True)


def sum_over_ka(payload):
    parts = lax.all_to_all(payload, "core", 1, 1, tiled=True)
    chip = jnp.sum(parts, axis=1)
    parts = lax.all_to_all(chip, "zl", 0, 0, tiled=True)
    return jnp.sum(parts, axis=0)


def sum_over_all(values):
    pair = jnp.broadcast_to(values[None, :], (lax.axis_size("core"), values.shape[0]))
    chip = jnp.sum(lax.all_to_all(pair, "core", 0, 0, tiled=True), axis=0)
    chips = 1
    for axis in ALL_AXES[:-1]:
        chips *= lax.axis_size(axis)
    copies = jnp.broadcast_to(chip[None, :], (chips, values.shape[0]))
    return jnp.sum(lax.all_to_all(copies, ALL_AXES[:-1], 0, 0, tiled=True), axis=0)


def local(
    features,
    positions,
    k_indices,
    species,
    brick_counts,
    smearing,
    teacher_charge,
    norm_gain,
    w_mix,
    w_read,
    w_student,
    species_embed,
    w_charge,
    species_bias,
    student_smear,
):
    atom_rows = features.shape[0]
    k_width = k_indices.shape[1]
    channels = features.shape[1]
    atom_groups = 1
    for axis in ATOM_AXES:
        atom_groups *= lax.axis_size(axis)
    ka_groups = 1
    for axis in KA_AXES:
        ka_groups *= lax.axis_size(axis)
    inv_root = 1.0 / math.sqrt(atom_rows * atom_groups)
    live_mask = (jnp.arange(atom_rows, dtype=jnp.int32) < brick_counts[0]).astype(jnp.float32)
    masked = features * live_mask.astype(jnp.bfloat16)[:, None]
    charge = student_charge(
        features, species, live_mask, w_student, species_embed, w_charge, species_bias
    )
    charge_low = charge.astype(jnp.bfloat16)
    phases = lax.optimization_barrier(phase_table(positions, k_indices))
    factor = lax.dot_general(
        phases, masked, (((0,), (0,)), ((), ())), preferred_element_type=jnp.float32
    )
    charge_sum = jnp.dot(charge_low, phases, preferred_element_type=jnp.float32)
    rows_each = 2 * k_width // atom_groups
    flat = rows_each * channels
    payload = jnp.concatenate(
        [factor.reshape(atom_groups, flat), charge_sum.reshape(atom_groups, rows_each)], axis=1
    )
    k_vectors, k_square = k_geometry(k_indices)
    owner = lax.axis_index(ATOM_AXES)
    k_start = (owner * rows_each) % k_width

    def weigh(chunk):
        chunk_square = lax.dynamic_slice_in_dim(k_square, k_start, rows_each, 0)
        chunk_kernel = teacher_kernel(chunk_square, smearing, inv_root)
        rows = chunk[:flat].reshape(rows_each, channels)
        rounded = (chunk_kernel * rows).astype(jnp.bfloat16).astype(jnp.float32)
        return jnp.concatenate([rounded.reshape(-1), chunk[flat:]])

    summed = sum_over_atoms(payload, weigh)
    weighted = summed[:, :flat].reshape(2 * k_width, channels).astype(jnp.bfloat16)
    charge_sum = summed[:, flat:].reshape(-1)
    potential = jnp.dot(phases, weighted, preferred_element_type=jnp.float32)
    charged = (features.astype(jnp.float32) * teacher_charge[None, :]).astype(jnp.bfloat16)
    contracted = lax.dot_general(
        charged, weighted, (((1,), (1,)), ((), ())), preferred_element_type=jnp.float32
    )
    cosines = phases[:, :k_width].astype(jnp.float32)
    sines = phases[:, k_width:].astype(jnp.float32)
    force_terms = sines * contracted[:, :k_width] - cosines * contracted[:, k_width:]
    terms_high = force_terms.astype(jnp.bfloat16)
    terms_low = (force_terms - terms_high.astype(jnp.float32)).astype(jnp.bfloat16)
    k_low = k_indices.astype(jnp.bfloat16)
    terms = jnp.concatenate([terms_high, terms_low], axis=1)
    teacher_force_t = TWO_PI * lax.dot_general(
        jnp.concatenate([k_low, k_low], axis=1),
        terms,
        (((1,), (1,)), ((), ())),
        preferred_element_type=jnp.float32,
    )
    table = student_table(k_vectors, k_square, charge_sum, student_smear, inv_root, k_width)
    student_part_t = lax.dot_general(
        table, phases, (((0,), (1,)), ((), ())), preferred_element_type=jnp.float32
    )
    share_rows = atom_rows // ka_groups
    side = jnp.concatenate(
        [teacher_force_t, student_part_t, jnp.zeros((1, atom_rows), jnp.float32)], axis=0
    )
    side = side.reshape(8, ka_groups, share_rows).transpose(1, 0, 2)
    packed = jnp.concatenate([potential.reshape(ka_groups, share_rows, channels), side], axis=1)
    z_lo = lax.axis_size("zl")
    packed = packed.reshape(z_lo, ka_groups // z_lo, share_rows + 8, channels)
    own = sum_over_ka(packed)
    ka_index = lax.axis_index(KA_AXES)
    row_start = ka_index * share_rows

    def own_rows(values):
        return lax.dynamic_slice_in_dim(values, row_start, share_rows, 0)

    own_side = own[share_rows:].T
    teacher_features, teacher_out, forces, student_energy, misfit = finish(
        own[:share_rows],
        own_side[:, 0:3],
        own_side[:, 3:7],
        own_rows(features),
        own_rows(charge),
        own_rows(live_mask),
        norm_gain,
        w_mix,
        w_read,
    )
    totals = sum_over_all(jnp.stack([jnp.sum(misfit), jnp.sum(own_rows(live_mask))]))
    return (teacher_features, teacher_out.T, forces.T, student_energy, totals[0] / totals[1])


def solution(mesh):
    sizes = dict(mesh.shape)
    ka = sizes["ka"]
    atom = sizes["atom"]
    cores = 2
    z_lo = ka // cores
    devices = mesh.devices.reshape(-1)
    y_size = 8 if atom % 8 == 0 else 1
    rest = atom // y_size
    zh = 2 if rest % 2 == 0 else 1
    x_size = rest // zh
    fine = Mesh(devices.reshape(y_size, x_size, zh, z_lo, cores), ALL_AXES)
    atom_spec = ATOM_AXES
    in_specs = (
        P(atom_spec, None),
        P(None, atom_spec),
        P(None, KA_AXES),
        P(atom_spec),
        P(atom_spec),
        P(),
        P(),
        P(),
        P(),
        P(),
        P(),
        P(),
        P(),
        P(),
        P(),
    )
    out_specs = (
        P(ALL_AXES, None),
        P(None, ALL_AXES),
        P(None, ALL_AXES),
        P(ALL_AXES),
        P(),
    )
    return jax.shard_map(local, mesh=fine, in_specs=in_specs, out_specs=out_specs, check_vma=False)
```

```python
import math

import jax
import jax.numpy as jnp
from jax import lax
from jax.sharding import Mesh
from jax.sharding import PartitionSpec as P

TWO_PI = 2.0 * math.pi
SCREEN = 20.0
HIGHEST_PRECISION = lax.Precision.HIGHEST

ATOM_AXES = ("y", "x", "zh")
KA_AXES = ("zl", "core")
ALL_AXES = ATOM_AXES + KA_AXES


def phase_table(positions, k_indices):
    k_float = k_indices.astype(jnp.float32)
    products = (
        positions[0][:, None] * k_float[0][None, :]
        + positions[1][:, None] * k_float[1][None, :]
        + positions[2][:, None] * k_float[2][None, :]
    )
    quarters = 4.0 * products
    quarter = jnp.round(quarters)
    angle = (quarters - quarter) * (0.5 * math.pi)
    square = angle * angle
    sine = angle * (
        1.0
        + square
        * (
            -1.0 / 6.0
            + square * (1.0 / 120.0 + square * (-1.0 / 5040.0 + square * (1.0 / 362880.0)))
        )
    )
    cosine = 1.0 + square * (
        -0.5 + square * (1.0 / 24.0 + square * (-1.0 / 720.0 + square * (1.0 / 40320.0)))
    )
    turn = quarter - 4.0 * jnp.floor(quarter * 0.25)
    odd = (turn == 1.0) | (turn == 3.0)
    cos_base = jnp.where(odd, sine, cosine)
    sin_base = jnp.where(odd, cosine, sine)
    cos_value = jnp.where((turn == 1.0) | (turn == 2.0), -cos_base, cos_base)
    sin_value = jnp.where(turn >= 2.0, -sin_base, sin_base)
    return jnp.concatenate([cos_value, sin_value], axis=1).astype(jnp.bfloat16)


def k_geometry(k_indices):
    k_vectors = TWO_PI * k_indices.astype(jnp.float32)
    k_square = (
        k_vectors[0] * k_vectors[0] + k_vectors[1] * k_vectors[1] + k_vectors[2] * k_vectors[2]
    )
    return (k_vectors, k_square)


def teacher_kernel(k_square, smearing, inv_root):
    spread = (smearing * smearing)[None, :]
    return jnp.exp(-0.5 * k_square[:, None] * spread) / (k_square[:, None] + SCREEN) * inv_root


def student_table(k_vectors, k_square, sums, student_smear, inv_root, k_width):
    spread = student_smear[0] * student_smear[0]
    kernel = jnp.exp(-0.5 * k_square * spread) / (k_square + SCREEN) * inv_root
    cos_part = kernel * sums[:k_width]
    sin_part = kernel * sums[k_width:]
    upper_rows = jnp.stack(
        [
            cos_part,
            -(k_vectors[0] * sin_part),
            -(k_vectors[1] * sin_part),
            -(k_vectors[2] * sin_part),
        ],
        axis=1,
    )
    lower_rows = jnp.stack(
        [sin_part, k_vectors[0] * cos_part, k_vectors[1] * cos_part, k_vectors[2] * cos_part],
        axis=1,
    )
    return jnp.concatenate([upper_rows, lower_rows], axis=0).astype(jnp.bfloat16)


def student_charge(features, species, live_mask, w_student, species_embed, w_charge, species_bias):
    onehot = (
        species[:, None] == jnp.arange(species_embed.shape[0], dtype=jnp.int32)[None, :]
    ).astype(jnp.float32)
    inner_sum = jnp.dot(features, w_student, preferred_element_type=jnp.float32) + jnp.dot(
        onehot, species_embed, precision=HIGHEST_PRECISION
    )
    hidden = jax.nn.silu(inner_sum)
    return (
        jnp.sum(hidden * w_charge[None, :], axis=1)
        + jnp.dot(onehot, species_bias, precision=HIGHEST_PRECISION)
    ) * live_mask


def finish(
    potential, teacher_force, student_part, features, charge, live_mask, norm_gain, w_mix, w_read
):
    mean_square = jnp.mean(potential * potential, axis=1, keepdims=True)
    normed = (potential * lax.rsqrt(mean_square + 1e-06) * norm_gain[None, :]).astype(jnp.bfloat16)
    update = jax.nn.silu(jnp.dot(normed, w_mix, preferred_element_type=jnp.float32))
    combined = features.astype(jnp.float32) + update
    teacher_energy = jnp.sum(combined * w_read[None, :], axis=1)
    student_energy = 0.5 * charge * student_part[:, 0]
    forces = charge[:, None] * student_part[:, 1:4]
    misfit = (student_energy - teacher_energy) ** 2 + jnp.sum(
        (forces - teacher_force) ** 2, axis=1
    ) / 3.0
    return (
        combined.astype(jnp.bfloat16),
        teacher_force,
        forces,
        student_energy,
        live_mask * misfit,
    )


def sum_over_atoms(payload, finish_chunk):
    parts = lax.all_to_all(payload, ATOM_AXES, 0, 0, tiled=True)
    reduced = finish_chunk(jnp.sum(parts, axis=0))
    spread = jnp.broadcast_to(reduced[None, :], payload.shape)
    return lax.all_to_all(spread, ATOM_AXES, 0, 0, tiled=True)


def sum_over_ka(payload):
    parts = lax.all_to_all(payload, "core", 1, 1, tiled=True)
    chip = jnp.sum(parts, axis=1)
    parts = lax.all_to_all(chip, "zl", 0, 0, tiled=True)
    return jnp.sum(parts, axis=0)


def sum_over_all(values):
    pair = jnp.broadcast_to(values[None, :], (lax.axis_size("core"), values.shape[0]))
    chip = jnp.sum(lax.all_to_all(pair, "core", 0, 0, tiled=True), axis=0)
    chips = 1
    for axis in ALL_AXES[:-1]:
        chips *= lax.axis_size(axis)
    copies = jnp.broadcast_to(chip[None, :], (chips, values.shape[0]))
    return jnp.sum(lax.all_to_all(copies, ALL_AXES[:-1], 0, 0, tiled=True), axis=0)


def local(
    features,
    positions,
    k_indices,
    species,
    brick_counts,
    smearing,
    teacher_charge,
    norm_gain,
    w_mix,
    w_read,
    w_student,
    species_embed,
    w_charge,
    species_bias,
    student_smear,
):
    atom_rows = features.shape[0]
    k_width = k_indices.shape[1]
    channels = features.shape[1]
    atom_groups = 1
    for axis in ATOM_AXES:
        atom_groups *= lax.axis_size(axis)
    ka_groups = 1
    for axis in KA_AXES:
        ka_groups *= lax.axis_size(axis)
    inv_root = 1.0 / math.sqrt(atom_rows * atom_groups)
    live_mask = (jnp.arange(atom_rows, dtype=jnp.int32) < brick_counts[0]).astype(jnp.float32)
    masked = features * live_mask.astype(jnp.bfloat16)[:, None]
    charge = student_charge(
        features, species, live_mask, w_student, species_embed, w_charge, species_bias
    )
    charge_low = charge.astype(jnp.bfloat16)
    phases = lax.optimization_barrier(phase_table(positions, k_indices))
    factor = lax.dot_general(
        phases, masked, (((0,), (0,)), ((), ())), preferred_element_type=jnp.float32
    )
    charge_sum = jnp.dot(charge_low, phases, preferred_element_type=jnp.float32)
    rows_each = 2 * k_width // atom_groups
    flat = rows_each * channels
    payload = jnp.concatenate(
        [factor.reshape(atom_groups, flat), charge_sum.reshape(atom_groups, rows_each)], axis=1
    )
    k_vectors, k_square = k_geometry(k_indices)
    owner = lax.axis_index(ATOM_AXES)
    k_start = (owner * rows_each) % k_width

    def weigh(chunk):
        chunk_square = lax.dynamic_slice_in_dim(k_square, k_start, rows_each, 0)
        chunk_kernel = teacher_kernel(chunk_square, smearing, inv_root)
        rows = chunk[:flat].reshape(rows_each, channels)
        rounded = (chunk_kernel * rows).astype(jnp.bfloat16).astype(jnp.float32)
        return jnp.concatenate([rounded.reshape(-1), chunk[flat:]])

    summed = sum_over_atoms(payload, weigh)
    weighted = summed[:, :flat].reshape(2 * k_width, channels).astype(jnp.bfloat16)
    charge_sum = summed[:, flat:].reshape(-1)
    potential = jnp.dot(phases, weighted, preferred_element_type=jnp.float32)
    charged = (features.astype(jnp.float32) * teacher_charge[None, :]).astype(jnp.bfloat16)
    contracted = lax.dot_general(
        charged, weighted, (((1,), (1,)), ((), ())), preferred_element_type=jnp.float32
    )
    cosines = phases[:, :k_width].astype(jnp.float32)
    sines = phases[:, k_width:].astype(jnp.float32)
    force_terms = sines * contracted[:, :k_width] - cosines * contracted[:, k_width:]
    terms_high = force_terms.astype(jnp.bfloat16)
    terms_low = (force_terms - terms_high.astype(jnp.float32)).astype(jnp.bfloat16)
    k_low = k_indices.astype(jnp.bfloat16)
    terms = jnp.concatenate([terms_high, terms_low], axis=1)
    teacher_force_t = TWO_PI * lax.dot_general(
        jnp.concatenate([k_low, k_low], axis=1),
        terms,
        (((1,), (1,)), ((), ())),
        preferred_element_type=jnp.float32,
    )
    table = student_table(k_vectors, k_square, charge_sum, student_smear, inv_root, k_width)
    student_part_t = lax.dot_general(
        table, phases, (((0,), (1,)), ((), ())), preferred_element_type=jnp.float32
    )
    share_rows = atom_rows // ka_groups
    side = jnp.concatenate(
        [teacher_force_t, student_part_t, jnp.zeros((1, atom_rows), jnp.float32)], axis=0
    )
    side = side.reshape(8, ka_groups, share_rows).transpose(1, 0, 2)
    packed = jnp.concatenate([potential.reshape(ka_groups, share_rows, channels), side], axis=1)
    z_lo = lax.axis_size("zl")
    packed = packed.reshape(z_lo, ka_groups // z_lo, share_rows + 8, channels)
    own = sum_over_ka(packed)
    ka_index = lax.axis_index(KA_AXES)
    row_start = ka_index * share_rows

    def own_rows(values):
        return lax.dynamic_slice_in_dim(values, row_start, share_rows, 0)

    own_side = own[share_rows:].T
    teacher_features, teacher_out, forces, student_energy, misfit = finish(
        own[:share_rows],
        own_side[:, 0:3],
        own_side[:, 3:7],
        own_rows(features),
        own_rows(charge),
        own_rows(live_mask),
        norm_gain,
        w_mix,
        w_read,
    )
    totals = sum_over_all(jnp.stack([jnp.sum(misfit), jnp.sum(own_rows(live_mask))]))
    return (teacher_features, teacher_out.T, forces.T, student_energy, totals[0] / totals[1])


def solution(mesh):
    sizes = dict(mesh.shape)
    ka = sizes["ka"]
    atom = sizes["atom"]
    cores = 2
    z_lo = ka // cores
    devices = mesh.devices.reshape(-1)
    y_size = 8 if atom % 8 == 0 else 1
    rest = atom // y_size
    zh = 2 if rest % 2 == 0 else 1
    x_size = rest // zh
    fine = Mesh(devices.reshape(y_size, x_size, zh, z_lo, cores), ALL_AXES)
    atom_spec = ATOM_AXES
    in_specs = (
        P(atom_spec, None),
        P(None, atom_spec),
        P(None, KA_AXES),
        P(atom_spec),
        P(atom_spec),
        P(),
        P(),
        P(),
        P(),
        P(),
        P(),
        P(),
        P(),
        P(),
        P(),
    )
    out_specs = (
        P(ALL_AXES, None),
        P(None, ALL_AXES),
        P(None, ALL_AXES),
        P(ALL_AXES),
        P(),
    )
    return jax.shard_map(local, mesh=fine, in_specs=in_specs, out_specs=out_specs, check_vma=False)
```

```python
import math

import jax
import jax.numpy as jnp
from jax import lax
from jax.sharding import Mesh
from jax.sharding import PartitionSpec as P

TWO_PI = 2.0 * math.pi
SCREEN = 20.0
HIGHEST_PRECISION = lax.Precision.HIGHEST

ATOM_AXES = ("y", "x", "zh")
KA_AXES = ("zl", "core")
ALL_AXES = ATOM_AXES + KA_AXES


def phase_table(positions, k_indices):
    k_float = k_indices.astype(jnp.float32)
    products = (
        positions[0][:, None] * k_float[0][None, :]
        + positions[1][:, None] * k_float[1][None, :]
        + positions[2][:, None] * k_float[2][None, :]
    )
    quarters = 4.0 * products
    quarter = jnp.round(quarters)
    angle = (quarters - quarter) * (0.5 * math.pi)
    square = angle * angle
    sine = angle * (
        1.0
        + square
        * (
            -1.0 / 6.0
            + square * (1.0 / 120.0 + square * (-1.0 / 5040.0 + square * (1.0 / 362880.0)))
        )
    )
    cosine = 1.0 + square * (
        -0.5 + square * (1.0 / 24.0 + square * (-1.0 / 720.0 + square * (1.0 / 40320.0)))
    )
    turn = quarter - 4.0 * jnp.floor(quarter * 0.25)
    odd = (turn == 1.0) | (turn == 3.0)
    cos_base = jnp.where(odd, sine, cosine)
    sin_base = jnp.where(odd, cosine, sine)
    cos_value = jnp.where((turn == 1.0) | (turn == 2.0), -cos_base, cos_base)
    sin_value = jnp.where(turn >= 2.0, -sin_base, sin_base)
    return jnp.concatenate([cos_value, sin_value], axis=1).astype(jnp.bfloat16)


def k_geometry(k_indices):
    k_vectors = TWO_PI * k_indices.astype(jnp.float32)
    k_square = (
        k_vectors[0] * k_vectors[0] + k_vectors[1] * k_vectors[1] + k_vectors[2] * k_vectors[2]
    )
    return (k_vectors, k_square)


def teacher_kernel(k_square, smearing, inv_root):
    spread = (smearing * smearing)[None, :]
    return jnp.exp(-0.5 * k_square[:, None] * spread) / (k_square[:, None] + SCREEN) * inv_root


def student_table(k_vectors, k_square, sums, student_smear, inv_root, k_width):
    spread = student_smear[0] * student_smear[0]
    kernel = jnp.exp(-0.5 * k_square * spread) / (k_square + SCREEN) * inv_root
    cos_part = kernel * sums[:k_width]
    sin_part = kernel * sums[k_width:]
    upper_rows = jnp.stack(
        [
            cos_part,
            -(k_vectors[0] * sin_part),
            -(k_vectors[1] * sin_part),
            -(k_vectors[2] * sin_part),
        ],
        axis=1,
    )
    lower_rows = jnp.stack(
        [sin_part, k_vectors[0] * cos_part, k_vectors[1] * cos_part, k_vectors[2] * cos_part],
        axis=1,
    )
    return jnp.concatenate([upper_rows, lower_rows], axis=0).astype(jnp.bfloat16)


def student_charge(features, species, live_mask, w_student, species_embed, w_charge, species_bias):
    onehot = (
        species[:, None] == jnp.arange(species_embed.shape[0], dtype=jnp.int32)[None, :]
    ).astype(jnp.float32)
    inner_sum = jnp.dot(features, w_student, preferred_element_type=jnp.float32) + jnp.dot(
        onehot, species_embed, precision=HIGHEST_PRECISION
    )
    hidden = jax.nn.silu(inner_sum)
    return (
        jnp.sum(hidden * w_charge[None, :], axis=1)
        + jnp.dot(onehot, species_bias, precision=HIGHEST_PRECISION)
    ) * live_mask


def finish(
    potential, teacher_force, student_part, features, charge, live_mask, norm_gain, w_mix, w_read
):
    mean_square = jnp.mean(potential * potential, axis=1, keepdims=True)
    normed = (potential * lax.rsqrt(mean_square + 1e-06) * norm_gain[None, :]).astype(jnp.bfloat16)
    update = jax.nn.silu(jnp.dot(normed, w_mix, preferred_element_type=jnp.float32))
    combined = features.astype(jnp.float32) + update
    teacher_energy = jnp.sum(combined * w_read[None, :], axis=1)
    student_energy = 0.5 * charge * student_part[:, 0]
    forces = charge[:, None] * student_part[:, 1:4]
    misfit = (student_energy - teacher_energy) ** 2 + jnp.sum(
        (forces - teacher_force) ** 2, axis=1
    ) / 3.0
    return (
        combined.astype(jnp.bfloat16),
        teacher_force,
        forces,
        student_energy,
        live_mask * misfit,
    )


def sum_over_atoms(payload, finish_chunk):
    parts = lax.all_to_all(payload, ATOM_AXES, 0, 0, tiled=True)
    reduced = finish_chunk(jnp.sum(parts, axis=0))
    spread = jnp.broadcast_to(reduced[None, :], payload.shape)
    return lax.all_to_all(spread, ATOM_AXES, 0, 0, tiled=True)


def sum_over_ka(payload):
    parts = lax.all_to_all(payload, "core", 1, 1, tiled=True)
    chip = jnp.sum(parts, axis=1)
    parts = lax.all_to_all(chip, "zl", 0, 0, tiled=True)
    return jnp.sum(parts, axis=0)


def sum_over_all(values):
    devices = 1
    for axis in ALL_AXES:
        devices *= lax.axis_size(axis)
    copies = jnp.broadcast_to(values[None, :], (devices, values.shape[0]))
    return jnp.sum(lax.all_to_all(copies, ALL_AXES, 0, 0, tiled=True), axis=0)


def local(
    features,
    positions,
    k_indices,
    species,
    brick_counts,
    smearing,
    teacher_charge,
    norm_gain,
    w_mix,
    w_read,
    w_student,
    species_embed,
    w_charge,
    species_bias,
    student_smear,
):
    atom_rows = features.shape[0]
    k_width = k_indices.shape[1]
    channels = features.shape[1]
    atom_groups = 1
    for axis in ATOM_AXES:
        atom_groups *= lax.axis_size(axis)
    ka_groups = 1
    for axis in KA_AXES:
        ka_groups *= lax.axis_size(axis)
    inv_root = 1.0 / math.sqrt(atom_rows * atom_groups)
    live_mask = (jnp.arange(atom_rows, dtype=jnp.int32) < brick_counts[0]).astype(jnp.float32)
    masked = features * live_mask.astype(jnp.bfloat16)[:, None]
    charge = student_charge(
        features, species, live_mask, w_student, species_embed, w_charge, species_bias
    )
    charge_low = charge.astype(jnp.bfloat16)
    phases = lax.optimization_barrier(phase_table(positions, k_indices))
    factor = lax.dot_general(
        phases, masked, (((0,), (0,)), ((), ())), preferred_element_type=jnp.float32
    )
    charge_sum = jnp.dot(charge_low, phases, preferred_element_type=jnp.float32)
    rows_each = 2 * k_width // atom_groups
    flat = rows_each * channels
    payload = jnp.concatenate(
        [factor.reshape(atom_groups, flat), charge_sum.reshape(atom_groups, rows_each)], axis=1
    )
    k_vectors, k_square = k_geometry(k_indices)
    owner = lax.axis_index(ATOM_AXES)
    k_start = (owner * rows_each) % k_width

    def weigh(chunk):
        chunk_square = lax.dynamic_slice_in_dim(k_square, k_start, rows_each, 0)
        chunk_kernel = teacher_kernel(chunk_square, smearing, inv_root)
        rows = chunk[:flat].reshape(rows_each, channels)
        rounded = (chunk_kernel * rows).astype(jnp.bfloat16).astype(jnp.float32)
        return jnp.concatenate([rounded.reshape(-1), chunk[flat:]])

    summed = sum_over_atoms(payload, weigh)
    weighted = summed[:, :flat].reshape(2 * k_width, channels).astype(jnp.bfloat16)
    charge_sum = summed[:, flat:].reshape(-1)
    potential = jnp.dot(phases, weighted, preferred_element_type=jnp.float32)
    charged = (features.astype(jnp.float32) * teacher_charge[None, :]).astype(jnp.bfloat16)
    contracted = lax.dot_general(
        charged, weighted, (((1,), (1,)), ((), ())), preferred_element_type=jnp.float32
    )
    cosines = phases[:, :k_width].astype(jnp.float32)
    sines = phases[:, k_width:].astype(jnp.float32)
    force_terms = sines * contracted[:, :k_width] - cosines * contracted[:, k_width:]
    terms_high = force_terms.astype(jnp.bfloat16)
    terms_low = (force_terms - terms_high.astype(jnp.float32)).astype(jnp.bfloat16)
    k_low = k_indices.astype(jnp.bfloat16)
    terms = jnp.concatenate([terms_high, terms_low], axis=1)
    teacher_force_t = TWO_PI * lax.dot_general(
        jnp.concatenate([k_low, k_low], axis=1),
        terms,
        (((1,), (1,)), ((), ())),
        preferred_element_type=jnp.float32,
    )
    table = student_table(k_vectors, k_square, charge_sum, student_smear, inv_root, k_width)
    student_part_t = lax.dot_general(
        table, phases, (((0,), (1,)), ((), ())), preferred_element_type=jnp.float32
    )
    share_rows = atom_rows // ka_groups
    side = jnp.concatenate(
        [teacher_force_t, student_part_t, jnp.zeros((1, atom_rows), jnp.float32)], axis=0
    )
    side = side.reshape(8, ka_groups, share_rows).transpose(1, 0, 2)
    packed = jnp.concatenate([potential.reshape(ka_groups, share_rows, channels), side], axis=1)
    z_lo = lax.axis_size("zl")
    packed = packed.reshape(z_lo, ka_groups // z_lo, share_rows + 8, channels)
    own = sum_over_ka(packed)
    ka_index = lax.axis_index(KA_AXES)
    row_start = ka_index * share_rows

    def own_rows(values):
        return lax.dynamic_slice_in_dim(values, row_start, share_rows, 0)

    own_side = own[share_rows:].T
    teacher_features, teacher_out, forces, student_energy, misfit = finish(
        own[:share_rows],
        own_side[:, 0:3],
        own_side[:, 3:7],
        own_rows(features),
        own_rows(charge),
        own_rows(live_mask),
        norm_gain,
        w_mix,
        w_read,
    )
    totals = sum_over_all(jnp.stack([jnp.sum(misfit), jnp.sum(own_rows(live_mask))]))
    return (teacher_features, teacher_out.T, forces.T, student_energy, totals[0] / totals[1])


def solution(mesh):
    sizes = dict(mesh.shape)
    ka = sizes["ka"]
    atom = sizes["atom"]
    cores = 2
    z_lo = ka // cores
    devices = mesh.devices.reshape(-1)
    y_size = 8 if atom % 8 == 0 else 1
    rest = atom // y_size
    zh = 2 if rest % 2 == 0 else 1
    x_size = rest // zh
    fine = Mesh(devices.reshape(y_size, x_size, zh, z_lo, cores), ALL_AXES)
    atom_spec = ATOM_AXES
    in_specs = (
        P(atom_spec, None),
        P(None, atom_spec),
        P(None, KA_AXES),
        P(atom_spec),
        P(atom_spec),
        P(),
        P(),
        P(),
        P(),
        P(),
        P(),
        P(),
        P(),
        P(),
        P(),
    )
    out_specs = (
        P(ALL_AXES, None),
        P(None, ALL_AXES),
        P(None, ALL_AXES),
        P(ALL_AXES),
        P(),
    )
    return jax.shard_map(local, mesh=fine, in_specs=in_specs, out_specs=out_specs, check_vma=False)
```
